32 devices in a mesh: wave: 4 (over y, core), lev: 4 (over z), cpl: 2 (over x).
Axes of the slice: x: 2, y: 2, z: 4, core: 2. Of those that a mesh axis runs over, the one named last changes fastest.
Arguments:
- spectral: bfloat16 [1280, 2, 4, 24, 1280], P('wave', None, None, 'lev'), may hold values from -0.125 to 0.125
- legendre: bfloat16 [1280, 16, 1280], P('wave', 'cpl'), may hold values from -0.15625 to 0.15625
- wavenumber: int32 [1280], replicated, may hold values from 0 to 1279, each once
- level_weight: float32 [24], P('lev'), may hold values from 0.1 to 1
- source_row: int32 [16], replicated, may hold values from 0 to 14
- row_weight: float32 [16], replicated, may hold values from 0.2 to 0.8
Outputs:
- ocean_flux: float32 [16, 4, 4320], P(('wave', 'cpl'), None, 'lev')
The draws below stay inside these ranges and needn't reach their ends.
All inputs are finite; a program needn't handle non-finite values.
Results may differ from the reference program's by a relative error of at most 0.0041.
Values may be sent and summed in bfloat16 or wider, within the bound.
No kernel may reach another device: no remote copies, remote signals or barrier semaphores. Data moves between devices by JAX's collectives and lax.ppermute only.
A program may use at most 192 MiB of HBM per device.

```python
import math
import jax
import jax.numpy as jnp
from jax import lax

M = 1280
NLON = 4320
FIELDS = 4
LEV = 24
LAT = 16


def draw_source_row(key, part):
    shuffled = jax.random.permutation(jax.random.fold_in(key, 11), LAT)
    offset = jax.random.randint(jax.random.fold_in(key, 12), (LAT,), 0, 2)
    return jnp.clip(shuffled - offset, 0, LAT - 2).astype(jnp.int32)


def block_scale(stream_key, shape, cuts, low, high):
    def one(position, blocks):
        steps = jax.random.uniform(jax.random.fold_in(jax.random.fold_in(stream_key, 6), position), (blocks,), jnp.float32, low / len(cuts), high / len(cuts))
        return jnp.repeat(jnp.exp(steps), shape[position] // blocks).reshape((-1,) + (1,) * (len(shape) - position - 1))

    loudness = one(*cuts[0])
    for cut in cuts[1:]:
        loudness = loudness * one(*cut)
    return loudness


def scatter_about(stream_key, extent, width, reach, pieces=(), kind=jnp.bfloat16):
    result = width * jax.random.normal(stream_key, extent, jnp.float32)
    if pieces:
        result = result * block_scale(stream_key, extent, pieces, -0.22, 0.18)
    return jnp.clip(result, -reach, reach).astype(kind)


def setup_inputs(seed: int = 0) -> dict:
    key_of = jax.random.split(jax.random.key(seed), 7)
    spectral = scatter_about(key_of[0], (M, 2, FIELDS, LEV, M), (2 * M) ** -0.5, 0.125, ((0, 4), (3, 4)))
    legendre = scatter_about(key_of[1], (M, LAT, M), M ** -0.5, 0.15625, ((0, 4), (1, 2)))
    wavenumber = jax.random.permutation(key_of[2], M).astype(jnp.int32)
    level_weight = jnp.clip(jnp.exp(math.log(1.0) - 2.3025851 * jax.random.uniform(key_of[3], (LEV,), jnp.float32) ** block_scale(key_of[3], (LEV,), ((0, 4),), -0.2, 0.2)), 0.1, 1.0)
    source_row = draw_source_row(jax.random.fold_in(key_of[6], 71), 0)
    row_weight = jnp.clip(jax.random.uniform(key_of[5], (LAT,), jnp.float32, 0.2, 0.8), 0.2, 0.8)
    return {"spectral": spectral, "legendre": legendre, "wavenumber": wavenumber, "level_weight": level_weight, "source_row": source_row, "row_weight": row_weight}


def fourier_table(wavenumber, first_lon, lon_count, lon_total):
    longitude = first_lon + jnp.arange(lon_count, dtype=jnp.int32)
    phase = wavenumber[:, None] * longitude[None, :] % lon_total
    angle = phase.astype(jnp.float32) * (2.0 * math.pi / lon_total)
    factor = jnp.where(wavenumber == 0, 1.0, 2.0).astype(jnp.float32)[:, None]
    return jnp.stack([factor * jnp.cos(angle), -factor * jnp.sin(angle)], axis=1).astype(jnp.bfloat16)

def surface_flux(grid_vals, level_weight):
    wind_speed = jnp.sqrt(grid_vals[..., 0, :, :] ** 2 + grid_vals[..., 1, :, :] ** 2 + 0.25)
    return lax.optimization_barrier(jnp.sum(level_weight[:, None] * wind_speed[..., None, :, :] * grid_vals, axis=-2))

def reference(spectral, legendre, wavenumber, level_weight, source_row, row_weight):
    channels = 2 * FIELDS * LEV
    coefficient_all = spectral.reshape(M, channels, M)

    def one_wave(item):
        coefficient, table_rows, wave_now = item
        keep_mask = jnp.arange(M, dtype=jnp.int32) < (M - wave_now).astype(jnp.int32)
        coefficient = jnp.where(keep_mask[None, :], coefficient, jnp.zeros_like(coefficient))
        return jnp.einsum('kj,lj->lk', coefficient.astype(jnp.float32), table_rows.astype(jnp.float32)).astype(jnp.bfloat16)
    spec_grid = lax.map(one_wave, (coefficient_all, legendre, wavenumber))
    lat_major = spec_grid.reshape(M, LAT, 2, FIELDS * LEV).transpose(1, 3, 0, 2).reshape(LAT, FIELDS * LEV, 2 * M)
    fourier = fourier_table(wavenumber, 0, NLON, NLON).reshape(2 * M, NLON)

    def one_lat(rows_in):
        grid_vals = jnp.dot(rows_in, fourier, preferred_element_type=jnp.float32).reshape(FIELDS, LEV, NLON)
        return surface_flux(grid_vals, level_weight)
    flux = lax.map(one_lat, lat_major)
    lower = jnp.take(flux, source_row, axis=0)
    upper = jnp.take(flux, source_row + 1, axis=0)
    weight_hi = row_weight[:, None, None]
    return (1.0 - weight_hi) * lower + weight_hi * upper
```

```python
import math

import jax
import jax.numpy as jnp
from jax import lax
from jax.sharding import PartitionSpec as P

NLON = 4320
LANE = 128


def phase_angle(phase, lon_total):
    return phase.astype(jnp.float32) * (2.0 * math.pi / lon_total)


def surface_flux(grid_vals, level_weight):
    wind_speed = jnp.sqrt(grid_vals[:, 0] ** 2 + grid_vals[:, 1] ** 2 + 0.25)
    return jnp.sum(level_weight[:, None] * wind_speed[:, None] * grid_vals, axis=2)


def latitude_order(gathered, wave_count, cpl_count, lat_dev):
    trailing = gathered.shape[1:]
    gathered = gathered.reshape((wave_count, cpl_count, lat_dev) + trailing)
    gathered = jnp.swapaxes(gathered, 0, 1)
    return gathered.reshape((wave_count * cpl_count * lat_dev,) + trailing)


def interpolate(gathered, source, weight_hi):
    lower = jnp.take(gathered, source, axis=0)
    upper = jnp.take(gathered, source + 1, axis=0)
    return (1.0 - weight_hi[:, None, None]) * lower + weight_hi[:, None, None] * upper


def quarter_tables(wavenumber, width):
    blocks = width // LANE
    factor = jnp.where(wavenumber == 0, 1.0, 2.0).astype(jnp.float32)[:, None]
    offsets = jnp.arange(LANE, dtype=jnp.int32)
    base_angle = phase_angle(wavenumber[:, None] * offsets[None, :] % NLON, NLON)
    base_cos = jnp.cos(base_angle)[:, None, :]
    base_sin = jnp.sin(base_angle)[:, None, :]
    starts = jnp.arange(blocks, dtype=jnp.int32) * LANE
    start_angle = phase_angle(wavenumber[:, None] * starts[None, :] % NLON, NLON)
    start_cos = (factor * jnp.cos(start_angle))[:, :, None]
    start_sin = (factor * jnp.sin(start_angle))[:, :, None]
    cos_tab = start_cos * base_cos - start_sin * base_sin
    sin_tab = start_sin * base_cos + start_cos * base_sin
    slots = wavenumber.shape[0]
    return (
        cos_tab.astype(jnp.bfloat16).reshape(slots, width),
        (-sin_tab).astype(jnp.bfloat16).reshape(slots, width),
    )


def local(spectral, legendre, wavenumber, level_weight, source_row, row_weight):
    slot_count = spectral.shape[0]
    fields = spectral.shape[2]
    levels = spectral.shape[3]
    degree = spectral.shape[4]
    channels = 2 * fields * levels
    wave_count = lax.axis_size("wave")
    cpl_count = lax.axis_size("cpl")
    lev_count = lax.axis_size("lev")
    wave_at = lax.axis_index("wave")
    cpl_at = lax.axis_index("cpl")
    owned_waves = lax.dynamic_slice_in_dim(wavenumber, wave_at * slot_count, slot_count)
    in_triangle = (
        lax.broadcasted_iota(jnp.int32, (slot_count, 1, degree), 2)
        < (degree - owned_waves)[:, None, None]
    )
    table_rows = jnp.where(in_triangle, legendre, jnp.zeros_like(legendre))
    coefficient = spectral.reshape(slot_count, channels, degree)
    spec_grid = jnp.einsum(
        "skj,slj->slk", coefficient, table_rows, preferred_element_type=jnp.float32
    ).astype(jnp.bfloat16)
    by_latitude = lax.all_to_all(spec_grid, "wave", split_axis=1, concat_axis=0, tiled=True)
    total_slots = by_latitude.shape[0]
    lat_dev = by_latitude.shape[1]
    rows = lat_dev * fields * levels
    parts = by_latitude.reshape(total_slots, lat_dev, 2, fields * levels)
    real = parts[:, :, 0].reshape(total_slots, rows).T
    imag = parts[:, :, 1].reshape(total_slots, rows).T
    parity = (1 - 2 * (wavenumber & 1)).astype(jnp.bfloat16)[None, :]
    lhs_cos = jnp.concatenate([real, real * parity], axis=0)
    lhs_sin = jnp.concatenate([imag, imag * parity], axis=0)

    quarter = NLON // 4
    width = -(-(quarter + 1) // LANE) * LANE
    cos_tab, sin_tab = quarter_tables(wavenumber, width)
    r_all = jnp.dot(lhs_cos, cos_tab, preferred_element_type=jnp.float32)
    q_all = jnp.dot(lhs_sin, sin_tab, preferred_element_type=jnp.float32)
    r1, r2 = r_all[:rows], r_all[rows:]
    q1, q2 = q_all[:rows], q_all[rows:]

    def flux_of(grid_rows):
        return surface_flux(grid_rows.reshape(lat_dev, fields, levels, quarter), level_weight)

    strip0 = flux_of((r1 + q1)[:, :quarter])
    strip1 = jnp.flip(flux_of((r2 - q2)[:, 1 : quarter + 1]), axis=-1)
    strip2 = flux_of((r2 + q2)[:, :quarter])
    strip3 = jnp.flip(flux_of((r1 - q1)[:, 1 : quarter + 1]), axis=-1)
    partial_value = jnp.concatenate([strip0, strip1, strip2, strip3], axis=-1)

    own_first = (wave_at * cpl_count + cpl_at) * lat_dev
    source = lax.dynamic_slice_in_dim(source_row, own_first, lat_dev)
    weight_hi = lax.dynamic_slice_in_dim(row_weight, own_first, lat_dev)
    summed = lax.psum_scatter(partial_value, "lev", scatter_dimension=2, tiled=True)
    gathered = lax.all_gather(summed, ("wave", "cpl"), axis=0, tiled=True)
    gathered = latitude_order(gathered, wave_count, cpl_count, lat_dev)
    del lev_count
    return interpolate(gathered, source, weight_hi)


def solution(mesh):
    placed = (P("wave", None, None, "lev", None), P("wave", "cpl", None), P(), P("lev"), P(), P())
    return jax.shard_map(
        local,
        mesh=mesh,
        in_specs=placed,
        out_specs=P(("wave", "cpl"), None, "lev"),
        check_vma=False,
    )
```

```python
import math

import jax
import jax.numpy as jnp
from jax import lax
from jax.sharding import PartitionSpec as P

NLON = 4320
LANE = 128


def phase_angle(phase, lon_total):
    return phase.astype(jnp.float32) * (2.0 * math.pi / lon_total)


def surface_flux(grid_vals, level_weight):
    wind_speed = jnp.sqrt(grid_vals[:, 0] ** 2 + grid_vals[:, 1] ** 2 + 0.25)
    return jnp.sum(level_weight[:, None] * wind_speed[:, None] * grid_vals, axis=2)


def latitude_order(gathered, wave_count, cpl_count, lat_dev):
    trailing = gathered.shape[1:]
    gathered = gathered.reshape((wave_count, cpl_count, lat_dev) + trailing)
    gathered = jnp.swapaxes(gathered, 0, 1)
    return gathered.reshape((wave_count * cpl_count * lat_dev,) + trailing)


def interpolate(gathered, source, weight_hi):
    lower = jnp.take(gathered, source, axis=0)
    upper = jnp.take(gathered, source + 1, axis=0)
    return (1.0 - weight_hi[:, None, None]) * lower + weight_hi[:, None, None] * upper


def quarter_tables(wavenumber, width):
    blocks = width // LANE
    factor = jnp.where(wavenumber == 0, 1.0, 2.0).astype(jnp.float32)[:, None]
    offsets = jnp.arange(LANE, dtype=jnp.int32)
    base_angle = phase_angle(wavenumber[:, None] * offsets[None, :] % NLON, NLON)
    base_cos = jnp.cos(base_angle)[:, None, :]
    base_sin = jnp.sin(base_angle)[:, None, :]
    starts = jnp.arange(blocks, dtype=jnp.int32) * LANE
    start_angle = phase_angle(wavenumber[:, None] * starts[None, :] % NLON, NLON)
    start_cos = (factor * jnp.cos(start_angle))[:, :, None]
    start_sin = (factor * jnp.sin(start_angle))[:, :, None]
    cos_tab = start_cos * base_cos - start_sin * base_sin
    sin_tab = start_sin * base_cos + start_cos * base_sin
    slots = wavenumber.shape[0]
    return (
        cos_tab.astype(jnp.bfloat16).reshape(slots, width),
        (-sin_tab).astype(jnp.bfloat16).reshape(slots, width),
    )


def local(spectral, legendre, wavenumber, level_weight, source_row, row_weight):
    slot_count = spectral.shape[0]
    fields = spectral.shape[2]
    levels = spectral.shape[3]
    degree = spectral.shape[4]
    channels = 2 * fields * levels
    wave_count = lax.axis_size("wave")
    cpl_count = lax.axis_size("cpl")
    lev_count = lax.axis_size("lev")
    wave_at = lax.axis_index("wave")
    cpl_at = lax.axis_index("cpl")
    owned_waves = lax.dynamic_slice_in_dim(wavenumber, wave_at * slot_count, slot_count)
    in_triangle = (
        lax.broadcasted_iota(jnp.int32, (slot_count, 1, degree), 2)
        < (degree - owned_waves)[:, None, None]
    )
    table_rows = jnp.where(in_triangle, legendre, jnp.zeros_like(legendre))
    coefficient = spectral.reshape(slot_count, channels, degree)
    spec_grid = jnp.einsum(
        "skj,slj->slk", coefficient, table_rows, preferred_element_type=jnp.float32
    ).astype(jnp.bfloat16)
    by_latitude = lax.all_to_all(spec_grid, "wave", split_axis=1, concat_axis=0, tiled=True)
    total_slots = by_latitude.shape[0]
    lat_dev = by_latitude.shape[1]
    rows = lat_dev * fields * levels
    parts = by_latitude.reshape(total_slots, lat_dev, 2, fields * levels)
    real = parts[:, :, 0].reshape(total_slots, rows).T
    imag = parts[:, :, 1].reshape(total_slots, rows).T
    parity = (1 - 2 * (wavenumber & 1)).astype(jnp.bfloat16)[None, :]
    lhs_cos = jnp.concatenate([real, real * parity], axis=0)
    lhs_sin = jnp.concatenate([imag, imag * parity], axis=0)

    quarter = NLON // 4
    width = -(-(quarter + 1) // LANE) * LANE
    cos_tab, sin_tab = quarter_tables(wavenumber, width)
    r_all = jnp.dot(lhs_cos, cos_tab, preferred_element_type=jnp.float32)
    q_all = jnp.dot(lhs_sin, sin_tab, preferred_element_type=jnp.float32)
    r1, r2 = r_all[:rows], r_all[rows:]
    q1, q2 = q_all[:rows], q_all[rows:]

    def flux_of(grid_rows):
        return surface_flux(grid_rows.reshape(lat_dev, fields, levels, quarter), level_weight)

    strip0 = flux_of((r1 + q1)[:, :quarter])
    strip1 = jnp.flip(flux_of((r2 - q2)[:, 1 : quarter + 1]), axis=-1)
    strip2 = flux_of((r2 + q2)[:, :quarter])
    strip3 = jnp.flip(flux_of((r1 - q1)[:, 1 : quarter + 1]), axis=-1)
    partial_value = jnp.concatenate([strip0, strip1, strip2, strip3], axis=-1)

    own_first = (wave_at * cpl_count + cpl_at) * lat_dev
    source = lax.dynamic_slice_in_dim(source_row, own_first, lat_dev)
    weight_hi = lax.dynamic_slice_in_dim(row_weight, own_first, lat_dev)
    strip_width = NLON // lev_count
    by_strip = partial_value.reshape(lat_dev, fields, lev_count, strip_width).transpose(2, 0, 1, 3)
    summed = jnp.sum(
        lax.all_to_all(by_strip, "lev", split_axis=0, concat_axis=0, tiled=True), axis=0
    )
    copies = jnp.broadcast_to(summed[None], (wave_count * cpl_count,) + summed.shape)
    gathered = lax.all_to_all(copies, ("wave", "cpl"), split_axis=0, concat_axis=0, tiled=True)
    gathered = gathered.reshape((wave_count * cpl_count * lat_dev,) + summed.shape[1:])
    gathered = latitude_order(gathered, wave_count, cpl_count, lat_dev)
    return interpolate(gathered, source, weight_hi)


def solution(mesh):
    placed = (P("wave", None, None, "lev", None), P("wave", "cpl", None), P(), P("lev"), P(), P())
    return jax.shard_map(
        local,
        mesh=mesh,
        in_specs=placed,
        out_specs=P(("wave", "cpl"), None, "lev"),
        check_vma=False,
    )
```

```python
import math

import jax
import jax.numpy as jnp
from jax import lax
from jax.sharding import PartitionSpec as P

NLON = 4320
LANE = 128


def phase_angle(phase, lon_total):
    return phase.astype(jnp.float32) * (2.0 * math.pi / lon_total)


def surface_flux(grid_vals, level_weight):
    wind_speed = jnp.sqrt(grid_vals[:, 0] ** 2 + grid_vals[:, 1] ** 2 + 0.25)
    return jnp.sum(level_weight[:, None] * wind_speed[:, None] * grid_vals, axis=2)


def latitude_order(gathered, wave_count, cpl_count, lat_dev):
    trailing = gathered.shape[1:]
    gathered = gathered.reshape((wave_count, cpl_count, lat_dev) + trailing)
    gathered = jnp.swapaxes(gathered, 0, 1)
    return gathered.reshape((wave_count * cpl_count * lat_dev,) + trailing)


def interpolate(gathered, source, weight_hi):
    lower = jnp.take(gathered, source, axis=0)
    upper = jnp.take(gathered, source + 1, axis=0)
    return (1.0 - weight_hi[:, None, None]) * lower + weight_hi[:, None, None] * upper


def quarter_tables(wavenumber, width):
    blocks = width // LANE
    factor = jnp.where(wavenumber == 0, 1.0, 2.0).astype(jnp.float32)[:, None]
    offsets = jnp.arange(LANE, dtype=jnp.int32)
    base_angle = phase_angle(wavenumber[:, None] * offsets[None, :] % NLON, NLON)
    base_cos = jnp.cos(base_angle)[:, None, :]
    base_sin = jnp.sin(base_angle)[:, None, :]
    starts = jnp.arange(blocks, dtype=jnp.int32) * LANE
    start_angle = phase_angle(wavenumber[:, None] * starts[None, :] % NLON, NLON)
    start_cos = (factor * jnp.cos(start_angle))[:, :, None]
    start_sin = (factor * jnp.sin(start_angle))[:, :, None]
    cos_tab = start_cos * base_cos - start_sin * base_sin
    sin_tab = start_sin * base_cos + start_cos * base_sin
    slots = wavenumber.shape[0]
    return (
        cos_tab.astype(jnp.bfloat16).reshape(slots, width),
        (-sin_tab).astype(jnp.bfloat16).reshape(slots, width),
    )


def local(spectral, legendre, wavenumber, level_weight, source_row, row_weight):
    slot_count = spectral.shape[0]
    fields = spectral.shape[2]
    levels = spectral.shape[3]
    degree = spectral.shape[4]
    channels = 2 * fields * levels
    wave_count = lax.axis_size("wave")
    cpl_count = lax.axis_size("cpl")
    lev_count = lax.axis_size("lev")
    wave_at = lax.axis_index("wave")
    cpl_at = lax.axis_index("cpl")
    owned_waves = lax.dynamic_slice_in_dim(wavenumber, wave_at * slot_count, slot_count)
    in_triangle = (
        lax.broadcasted_iota(jnp.int32, (slot_count, 1, degree), 2)
        < (degree - owned_waves)[:, None, None]
    )
    table_rows = jnp.where(in_triangle, legendre, jnp.zeros_like(legendre))
    stored = jnp.transpose(spectral, (0, 1, 3, 2, 4))
    spec_grid = jnp.einsum(
        "spafj,srj->srpfa", stored, table_rows, preferred_element_type=jnp.float32
    ).astype(jnp.bfloat16).reshape(slot_count, table_rows.shape[1], channels)
    by_latitude = lax.all_to_all(spec_grid, "wave", split_axis=1, concat_axis=0, tiled=True)
    total_slots = by_latitude.shape[0]
    lat_dev = by_latitude.shape[1]
    rows = lat_dev * fields * levels
    parts = by_latitude.reshape(total_slots, lat_dev, 2, fields * levels)
    real = parts[:, :, 0].reshape(total_slots, rows).T
    imag = parts[:, :, 1].reshape(total_slots, rows).T
    parity = (1 - 2 * (wavenumber & 1)).astype(jnp.bfloat16)[None, :]
    lhs_cos = jnp.concatenate([real, real * parity], axis=0)
    lhs_sin = jnp.concatenate([imag, imag * parity], axis=0)

    quarter = NLON // 4
    width = -(-(quarter + 1) // LANE) * LANE
    cos_tab, sin_tab = quarter_tables(wavenumber, width)
    r_all = jnp.dot(lhs_cos, cos_tab, preferred_element_type=jnp.float32)
    q_all = jnp.dot(lhs_sin, sin_tab, preferred_element_type=jnp.float32)
    r1, r2 = r_all[:rows], r_all[rows:]
    q1, q2 = q_all[:rows], q_all[rows:]

    def flux_of(grid_rows):
        return surface_flux(grid_rows.reshape(lat_dev, fields, levels, quarter), level_weight)

    strip0 = flux_of((r1 + q1)[:, :quarter])
    strip1 = jnp.flip(flux_of((r2 - q2)[:, 1 : quarter + 1]), axis=-1)
    strip2 = flux_of((r2 + q2)[:, :quarter])
    strip3 = jnp.flip(flux_of((r1 - q1)[:, 1 : quarter + 1]), axis=-1)
    partial_value = jnp.concatenate([strip0, strip1, strip2, strip3], axis=-1)

    own_first = (wave_at * cpl_count + cpl_at) * lat_dev
    source = lax.dynamic_slice_in_dim(source_row, own_first, lat_dev)
    weight_hi = lax.dynamic_slice_in_dim(row_weight, own_first, lat_dev)
    strip_width = NLON // lev_count
    by_strip = partial_value.reshape(lat_dev, fields, lev_count, strip_width).transpose(2, 0, 1, 3)
    summed = jnp.sum(
        lax.all_to_all(by_strip, "lev", split_axis=0, concat_axis=0, tiled=True), axis=0
    )
    copies = jnp.broadcast_to(summed[None], (wave_count * cpl_count,) + summed.shape)
    gathered = lax.all_to_all(copies, ("wave", "cpl"), split_axis=0, concat_axis=0, tiled=True)
    gathered = gathered.reshape((wave_count * cpl_count * lat_dev,) + summed.shape[1:])
    gathered = latitude_order(gathered, wave_count, cpl_count, lat_dev)
    return interpolate(gathered, source, weight_hi)


def solution(mesh):
    placed = (P("wave", None, None, "lev", None), P("wave", "cpl", None), P(), P("lev"), P(), P())
    return jax.shard_map(
        local,
        mesh=mesh,
        in_specs=placed,
        out_specs=P(("wave", "cpl"), None, "lev"),
        check_vma=False,
    )
```

```python
import math

import jax
import jax.numpy as jnp
from jax import lax
from jax.sharding import PartitionSpec as P
from jax.experimental import pallas as pl
from jax.experimental.pallas import tpu as pltpu

NLON = 4320
LANE = 128
SLOT_BLOCK = 8


def phase_angle(phase, lon_total):
    return phase.astype(jnp.float32) * (2.0 * math.pi / lon_total)


def surface_flux(grid_vals, level_weight):
    wind_speed = jnp.sqrt(grid_vals[:, 0] ** 2 + grid_vals[:, 1] ** 2 + 0.25)
    return jnp.sum(level_weight[:, None] * wind_speed[:, None] * grid_vals, axis=2)


def latitude_order(gathered, wave_count, cpl_count, lat_dev):
    trailing = gathered.shape[1:]
    gathered = gathered.reshape((wave_count, cpl_count, lat_dev) + trailing)
    gathered = jnp.swapaxes(gathered, 0, 1)
    return gathered.reshape((wave_count * cpl_count * lat_dev,) + trailing)


def interpolate(gathered, source, weight_hi):
    lower = jnp.take(gathered, source, axis=0)
    upper = jnp.take(gathered, source + 1, axis=0)
    return (1.0 - weight_hi[:, None, None]) * lower + weight_hi[:, None, None] * upper


def quarter_tables(wavenumber, width):
    blocks = width // LANE
    factor = jnp.where(wavenumber == 0, 1.0, 2.0).astype(jnp.float32)[:, None]
    offsets = jnp.arange(LANE, dtype=jnp.int32)
    base_angle = phase_angle(wavenumber[:, None] * offsets[None, :] % NLON, NLON)
    base_cos = jnp.cos(base_angle)[:, None, :]
    base_sin = jnp.sin(base_angle)[:, None, :]
    starts = jnp.arange(blocks, dtype=jnp.int32) * LANE
    start_angle = phase_angle(wavenumber[:, None] * starts[None, :] % NLON, NLON)
    start_cos = (factor * jnp.cos(start_angle))[:, :, None]
    start_sin = (factor * jnp.sin(start_angle))[:, :, None]
    cos_tab = start_cos * base_cos - start_sin * base_sin
    sin_tab = start_sin * base_cos + start_cos * base_sin
    slots = wavenumber.shape[0]
    return (
        cos_tab.astype(jnp.bfloat16).reshape(slots, width),
        (-sin_tab).astype(jnp.bfloat16).reshape(slots, width),
    )


def legendre_kernel(waves_ref, spec_ref, table_ref, out_ref):
    block = spec_ref.shape[0]
    degree = spec_ref.shape[-1]
    first = pl.program_id(0) * block

    def one_slot(s, carry):
        limit = degree - waves_ref[first + s]
        rows = table_ref[s]
        column = lax.broadcasted_iota(jnp.int32, rows.shape, 1)
        rows = jnp.where(column < limit, rows, jnp.zeros_like(rows))
        coefficient = spec_ref[s].reshape(-1, degree)
        out_ref[s] = lax.dot_general(
            rows, coefficient, (((1,), (1,)), ((), ())), preferred_element_type=jnp.float32
        ).astype(out_ref.dtype)
        return carry

    lax.fori_loop(0, block, one_slot, 0)


def legendre_transform(stored, legendre, owned_waves):
    slots, _, levels, fields, degree = stored.shape
    lats = legendre.shape[1]
    channels = 2 * levels * fields
    block = SLOT_BLOCK
    return pl.pallas_call(
        legendre_kernel,
        out_shape=jax.ShapeDtypeStruct((slots, lats, channels), jnp.bfloat16),
        grid_spec=pltpu.PrefetchScalarGridSpec(
            num_scalar_prefetch=1,
            grid=(slots // block,),
            in_specs=[
                pl.BlockSpec((block, 2, levels, fields, degree), lambda i, w: (i, 0, 0, 0, 0)),
                pl.BlockSpec((block, lats, degree), lambda i, w: (i, 0, 0)),
            ],
            out_specs=pl.BlockSpec((block, lats, channels), lambda i, w: (i, 0, 0)),
        ),
        cost_estimate=pl.CostEstimate(
            flops=2 * slots * lats * channels * degree,
            bytes_accessed=2 * slots * degree * (channels + lats),
            transcendentals=0,
        ),
    )(owned_waves, stored, legendre)


def local(spectral, legendre, wavenumber, level_weight, source_row, row_weight):
    slot_count = spectral.shape[0]
    fields = spectral.shape[2]
    levels = spectral.shape[3]
    degree = spectral.shape[4]
    channels = 2 * fields * levels
    wave_count = lax.axis_size("wave")
    cpl_count = lax.axis_size("cpl")
    lev_count = lax.axis_size("lev")
    wave_at = lax.axis_index("wave")
    cpl_at = lax.axis_index("cpl")
    owned_waves = lax.dynamic_slice_in_dim(wavenumber, wave_at * slot_count, slot_count)
    stored = jnp.transpose(spectral, (0, 1, 3, 2, 4))
    spec_grid = (
        legendre_transform(stored, legendre, owned_waves)
        .reshape(slot_count, legendre.shape[1], 2, levels, fields)
        .transpose(0, 1, 2, 4, 3)
        .reshape(slot_count, legendre.shape[1], channels)
    )
    by_latitude = lax.all_to_all(spec_grid, "wave", split_axis=1, concat_axis=0, tiled=True)
    total_slots = by_latitude.shape[0]
    lat_dev = by_latitude.shape[1]
    rows = lat_dev * fields * levels
    parts = by_latitude.reshape(total_slots, lat_dev, 2, fields * levels)
    real = parts[:, :, 0].reshape(total_slots, rows).T
    imag = parts[:, :, 1].reshape(total_slots, rows).T
    parity = (1 - 2 * (wavenumber & 1)).astype(jnp.bfloat16)[None, :]
    lhs_cos = jnp.concatenate([real, real * parity], axis=0)
    lhs_sin = jnp.concatenate([imag, imag * parity], axis=0)

    quarter = NLON // 4
    width = -(-(quarter + 1) // LANE) * LANE
    cos_tab, sin_tab = quarter_tables(wavenumber, width)
    r_all = jnp.dot(lhs_cos, cos_tab, preferred_element_type=jnp.float32)
    q_all = jnp.dot(lhs_sin, sin_tab, preferred_element_type=jnp.float32)
    r1, r2 = r_all[:rows], r_all[rows:]
    q1, q2 = q_all[:rows], q_all[rows:]

    def flux_of(grid_rows):
        return surface_flux(grid_rows.reshape(lat_dev, fields, levels, quarter), level_weight)

    strip0 = flux_of((r1 + q1)[:, :quarter])
    strip1 = jnp.flip(flux_of((r2 - q2)[:, 1 : quarter + 1]), axis=-1)
    strip2 = flux_of((r2 + q2)[:, :quarter])
    strip3 = jnp.flip(flux_of((r1 - q1)[:, 1 : quarter + 1]), axis=-1)
    partial_value = jnp.concatenate([strip0, strip1, strip2, strip3], axis=-1)

    own_first = (wave_at * cpl_count + cpl_at) * lat_dev
    source = lax.dynamic_slice_in_dim(source_row, own_first, lat_dev)
    weight_hi = lax.dynamic_slice_in_dim(row_weight, own_first, lat_dev)
    strip_width = NLON // lev_count
    by_strip = partial_value.reshape(lat_dev, fields, lev_count, strip_width).transpose(2, 0, 1, 3)
    summed = jnp.sum(
        lax.all_to_all(by_strip, "lev", split_axis=0, concat_axis=0, tiled=True), axis=0
    )
    copies = jnp.broadcast_to(summed[None], (wave_count * cpl_count,) + summed.shape)
    gathered = lax.all_to_all(copies, ("wave", "cpl"), split_axis=0, concat_axis=0, tiled=True)
    gathered = gathered.reshape((wave_count * cpl_count * lat_dev,) + summed.shape[1:])
    gathered = latitude_order(gathered, wave_count, cpl_count, lat_dev)
    return interpolate(gathered, source, weight_hi)


def solution(mesh):
    placed = (P("wave", None, None, "lev", None), P("wave", "cpl", None), P(), P("lev"), P(), P())
    return jax.shard_map(
        local,
        mesh=mesh,
        in_specs=placed,
        out_specs=P(("wave", "cpl"), None, "lev"),
        check_vma=False,
    )
```

```python
import math

import jax
import jax.numpy as jnp
from jax import lax
from jax.sharding import PartitionSpec as P
from jax.experimental import pallas as pl
from jax.experimental.pallas import tpu as pltpu

NLON = 4320
LANE = 128
SLOT_BLOCK = 8


def phase_angle(phase, lon_total):
    return phase.astype(jnp.float32) * (2.0 * math.pi / lon_total)


def surface_flux(grid_vals, level_weight):
    wind_speed = jnp.sqrt(grid_vals[:, 0] ** 2 + grid_vals[:, 1] ** 2 + 0.25)
    return jnp.sum(level_weight[:, None] * wind_speed[:, None] * grid_vals, axis=2)


def latitude_order(gathered, wave_count, cpl_count, lat_dev):
    trailing = gathered.shape[1:]
    gathered = gathered.reshape((wave_count, cpl_count, lat_dev) + trailing)
    gathered = jnp.swapaxes(gathered, 0, 1)
    return gathered.reshape((wave_count * cpl_count * lat_dev,) + trailing)


def interpolate(gathered, source, weight_hi):
    lower = jnp.take(gathered, source, axis=0)
    upper = jnp.take(gathered, source + 1, axis=0)
    return (1.0 - weight_hi[:, None, None]) * lower + weight_hi[:, None, None] * upper


def quarter_tables(wavenumber, width):
    blocks = width // LANE
    factor = jnp.where(wavenumber == 0, 1.0, 2.0).astype(jnp.float32)[:, None]
    offsets = jnp.arange(LANE, dtype=jnp.int32)
    base_angle = phase_angle(wavenumber[:, None] * offsets[None, :] % NLON, NLON)
    base_cos = jnp.cos(base_angle)[:, None, :]
    base_sin = jnp.sin(base_angle)[:, None, :]
    starts = jnp.arange(blocks, dtype=jnp.int32) * LANE
    start_angle = phase_angle(wavenumber[:, None] * starts[None, :] % NLON, NLON)
    start_cos = (factor * jnp.cos(start_angle))[:, :, None]
    start_sin = (factor * jnp.sin(start_angle))[:, :, None]
    cos_tab = start_cos * base_cos - start_sin * base_sin
    sin_tab = start_sin * base_cos + start_cos * base_sin
    slots = wavenumber.shape[0]
    return (
        cos_tab.astype(jnp.bfloat16).reshape(slots, width),
        (-sin_tab).astype(jnp.bfloat16).reshape(slots, width),
    )


def legendre_kernel(waves_ref, spec_ref, table_ref, out_ref):
    block = spec_ref.shape[0]
    degree = spec_ref.shape[-1]
    chunk = 256 if degree % 256 == 0 else LANE
    first = pl.program_id(0) * block

    def one_slot(s, carry):
        limit = degree - waves_ref[first + s]
        needed = (limit + chunk - 1) // chunk

        def one_chunk(c, total):
            start = pl.multiple_of(c * chunk, chunk)
            rows = table_ref[s, :, pl.ds(start, chunk)]
            column = start + lax.broadcasted_iota(jnp.int32, rows.shape, 1)
            rows = jnp.where(column < limit, rows, jnp.zeros_like(rows))
            coefficient = spec_ref[s, :, :, :, pl.ds(start, chunk)].reshape(-1, chunk)
            return total + lax.dot_general(
                rows, coefficient, (((1,), (1,)), ((), ())), preferred_element_type=jnp.float32
            )

        total = jnp.zeros(out_ref.shape[1:], jnp.float32)
        out_ref[s] = lax.fori_loop(0, needed, one_chunk, total).astype(out_ref.dtype)
        return carry

    lax.fori_loop(0, block, one_slot, 0)


def legendre_transform(stored, legendre, owned_waves):
    slots, _, levels, fields, degree = stored.shape
    lats = legendre.shape[1]
    channels = 2 * levels * fields
    block = SLOT_BLOCK
    return pl.pallas_call(
        legendre_kernel,
        out_shape=jax.ShapeDtypeStruct((slots, lats, channels), jnp.bfloat16),
        grid_spec=pltpu.PrefetchScalarGridSpec(
            num_scalar_prefetch=1,
            grid=(slots // block,),
            in_specs=[
                pl.BlockSpec((block, 2, levels, fields, degree), lambda i, w: (i, 0, 0, 0, 0)),
                pl.BlockSpec((block, lats, degree), lambda i, w: (i, 0, 0)),
            ],
            out_specs=pl.BlockSpec((block, lats, channels), lambda i, w: (i, 0, 0)),
        ),
        cost_estimate=pl.CostEstimate(
            flops=2 * slots * lats * channels * degree,
            bytes_accessed=2 * slots * degree * (channels + lats),
            transcendentals=0,
        ),
    )(owned_waves, stored, legendre)


def local(spectral, legendre, wavenumber, level_weight, source_row, row_weight):
    slot_count = spectral.shape[0]
    fields = spectral.shape[2]
    levels = spectral.shape[3]
    degree = spectral.shape[4]
    channels = 2 * fields * levels
    wave_count = lax.axis_size("wave")
    cpl_count = lax.axis_size("cpl")
    lev_count = lax.axis_size("lev")
    wave_at = lax.axis_index("wave")
    cpl_at = lax.axis_index("cpl")
    owned_waves = lax.dynamic_slice_in_dim(wavenumber, wave_at * slot_count, slot_count)
    stored = jnp.transpose(spectral, (0, 1, 3, 2, 4))
    spec_grid = (
        legendre_transform(stored, legendre, owned_waves)
        .reshape(slot_count, legendre.shape[1], 2, levels, fields)
        .transpose(0, 1, 2, 4, 3)
        .reshape(slot_count, legendre.shape[1], channels)
    )
    by_latitude = lax.all_to_all(spec_grid, "wave", split_axis=1, concat_axis=0, tiled=True)
    total_slots = by_latitude.shape[0]
    lat_dev = by_latitude.shape[1]
    rows = lat_dev * fields * levels
    parts = by_latitude.reshape(total_slots, lat_dev, 2, fields * levels)
    real = parts[:, :, 0].reshape(total_slots, rows).T
    imag = parts[:, :, 1].reshape(total_slots, rows).T
    parity = (1 - 2 * (wavenumber & 1)).astype(jnp.bfloat16)[None, :]
    lhs_cos = jnp.concatenate([real, real * parity], axis=0)
    lhs_sin = jnp.concatenate([imag, imag * parity], axis=0)

    quarter = NLON // 4
    width = -(-(quarter + 1) // LANE) * LANE
    cos_tab, sin_tab = quarter_tables(wavenumber, width)
    r_all = jnp.dot(lhs_cos, cos_tab, preferred_element_type=jnp.float32)
    q_all = jnp.dot(lhs_sin, sin_tab, preferred_element_type=jnp.float32)
    r1, r2 = r_all[:rows], r_all[rows:]
    q1, q2 = q_all[:rows], q_all[rows:]

    def flux_of(grid_rows):
        return surface_flux(grid_rows.reshape(lat_dev, fields, levels, quarter), level_weight)

    strip0 = flux_of((r1 + q1)[:, :quarter])
    strip1 = jnp.flip(flux_of((r2 - q2)[:, 1 : quarter + 1]), axis=-1)
    strip2 = flux_of((r2 + q2)[:, :quarter])
    strip3 = jnp.flip(flux_of((r1 - q1)[:, 1 : quarter + 1]), axis=-1)
    partial_value = jnp.concatenate([strip0, strip1, strip2, strip3], axis=-1)

    own_first = (wave_at * cpl_count + cpl_at) * lat_dev
    source = lax.dynamic_slice_in_dim(source_row, own_first, lat_dev)
    weight_hi = lax.dynamic_slice_in_dim(row_weight, own_first, lat_dev)
    strip_width = NLON // lev_count
    by_strip = partial_value.reshape(lat_dev, fields, lev_count, strip_width).transpose(2, 0, 1, 3)
    summed = jnp.sum(
        lax.all_to_all(by_strip, "lev", split_axis=0, concat_axis=0, tiled=True), axis=0
    )
    copies = jnp.broadcast_to(summed[None], (wave_count * cpl_count,) + summed.shape)
    gathered = lax.all_to_all(copies, ("wave", "cpl"), split_axis=0, concat_axis=0, tiled=True)
    gathered = gathered.reshape((wave_count * cpl_count * lat_dev,) + summed.shape[1:])
    gathered = latitude_order(gathered, wave_count, cpl_count, lat_dev)
    return interpolate(gathered, source, weight_hi)


def solution(mesh):
    placed = (P("wave", None, None, "lev", None), P("wave", "cpl", None), P(), P("lev"), P(), P())
    return jax.shard_map(
        local,
        mesh=mesh,
        in_specs=placed,
        out_specs=P(("wave", "cpl"), None, "lev"),
        check_vma=False,
    )
```

```python
import math

import jax
import jax.numpy as jnp
from jax import lax
from jax.sharding import PartitionSpec as P
from jax.experimental import pallas as pl
from jax.experimental.pallas import tpu as pltpu

NLON = 4320
LANE = 128
SLOT_BLOCK = 64


def phase_angle(phase, lon_total):
    return phase.astype(jnp.float32) * (2.0 * math.pi / lon_total)


def surface_flux(grid_vals, level_weight):
    wind_speed = jnp.sqrt(grid_vals[:, 0] ** 2 + grid_vals[:, 1] ** 2 + 0.25)
    return jnp.sum(level_weight[:, None] * wind_speed[:, None] * grid_vals, axis=2)


def latitude_order(gathered, wave_count, cpl_count, lat_dev):
    trailing = gathered.shape[1:]
    gathered = gathered.reshape((wave_count, cpl_count, lat_dev) + trailing)
    gathered = jnp.swapaxes(gathered, 0, 1)
    return gathered.reshape((wave_count * cpl_count * lat_dev,) + trailing)


def interpolate(gathered, source, weight_hi):
    lower = jnp.take(gathered, source, axis=0)
    upper = jnp.take(gathered, source + 1, axis=0)
    return (1.0 - weight_hi[:, None, None]) * lower + weight_hi[:, None, None] * upper


def quarter_tables(wavenumber, width):
    blocks = width // LANE
    factor = jnp.where(wavenumber == 0, 1.0, 2.0).astype(jnp.float32)[:, None]
    offsets = jnp.arange(LANE, dtype=jnp.int32)
    base_angle = phase_angle(wavenumber[:, None] * offsets[None, :] % NLON, NLON)
    base_cos = jnp.cos(base_angle)[:, None, :]
    base_sin = jnp.sin(base_angle)[:, None, :]
    starts = jnp.arange(blocks, dtype=jnp.int32) * LANE
    start_angle = phase_angle(wavenumber[:, None] * starts[None, :] % NLON, NLON)
    start_cos = (factor * jnp.cos(start_angle))[:, :, None]
    start_sin = (factor * jnp.sin(start_angle))[:, :, None]
    cos_tab = start_cos * base_cos - start_sin * base_sin
    sin_tab = start_sin * base_cos + start_cos * base_sin
    slots = wavenumber.shape[0]
    return (
        cos_tab.astype(jnp.bfloat16).reshape(slots, width),
        (-sin_tab).astype(jnp.bfloat16).reshape(slots, width),
    )


def legendre_kernel(waves_ref, spec_ref, table_ref, out_ref):
    block = spec_ref.shape[0]
    degree = spec_ref.shape[-1]
    first = pl.program_id(0) * block

    def one_slot(s, carry):
        limit = degree - waves_ref[first + s]
        rows = table_ref[s]
        column = lax.broadcasted_iota(jnp.int32, rows.shape, 1)
        rows = jnp.where(column < limit, rows, jnp.zeros_like(rows))
        coefficient = spec_ref[s].reshape(-1, degree)
        out_ref[s] = lax.dot_general(
            rows, coefficient, (((1,), (1,)), ((), ())), preferred_element_type=jnp.float32
        ).astype(out_ref.dtype)
        return carry

    lax.fori_loop(0, block, one_slot, 0, unroll=True)


def legendre_transform(stored, legendre, owned_waves):
    slots, _, levels, fields, degree = stored.shape
    lats = legendre.shape[1]
    channels = 2 * levels * fields
    block = max(b for b in range(1, SLOT_BLOCK + 1) if slots % b == 0)
    return pl.pallas_call(
        legendre_kernel,
        out_shape=jax.ShapeDtypeStruct((slots, lats, channels), jnp.bfloat16),
        grid_spec=pltpu.PrefetchScalarGridSpec(
            num_scalar_prefetch=1,
            grid=(slots // block,),
            in_specs=[
                pl.BlockSpec((block, 2, levels, fields, degree), lambda i, w: (i, 0, 0, 0, 0)),
                pl.BlockSpec((block, lats, degree), lambda i, w: (i, 0, 0)),
            ],
            out_specs=pl.BlockSpec((block, lats, channels), lambda i, w: (i, 0, 0)),
        ),
        cost_estimate=pl.CostEstimate(
            flops=2 * slots * lats * channels * degree,
            bytes_accessed=2 * slots * degree * (channels + lats),
            transcendentals=0,
        ),
    )(owned_waves, stored, legendre)


def local(spectral, legendre, wavenumber, level_weight, source_row, row_weight):
    slot_count = spectral.shape[0]
    fields = spectral.shape[2]
    levels = spectral.shape[3]
    degree = spectral.shape[4]
    channels = 2 * fields * levels
    wave_count = lax.axis_size("wave")
    cpl_count = lax.axis_size("cpl")
    lev_count = lax.axis_size("lev")
    wave_at = lax.axis_index("wave")
    cpl_at = lax.axis_index("cpl")
    owned_waves = lax.dynamic_slice_in_dim(wavenumber, wave_at * slot_count, slot_count)
    stored = jnp.transpose(spectral, (0, 1, 3, 2, 4))
    spec_grid = (
        legendre_transform(stored, legendre, owned_waves)
        .reshape(slot_count, legendre.shape[1], 2, levels, fields)
        .transpose(0, 1, 2, 4, 3)
        .reshape(slot_count, legendre.shape[1], channels)
    )
    by_latitude = lax.all_to_all(spec_grid, "wave", split_axis=1, concat_axis=0, tiled=True)
    total_slots = by_latitude.shape[0]
    lat_dev = by_latitude.shape[1]
    rows = lat_dev * fields * levels
    parts = by_latitude.reshape(total_slots, lat_dev, 2, fields * levels)
    real = parts[:, :, 0].reshape(total_slots, rows).T
    imag = parts[:, :, 1].reshape(total_slots, rows).T
    parity = (1 - 2 * (wavenumber & 1)).astype(jnp.bfloat16)[None, :]
    lhs_cos = jnp.concatenate([real, real * parity], axis=0)
    lhs_sin = jnp.concatenate([imag, imag * parity], axis=0)

    quarter = NLON // 4
    width = -(-(quarter + 1) // LANE) * LANE
    cos_tab, sin_tab = quarter_tables(wavenumber, width)
    r_all = jnp.dot(lhs_cos, cos_tab, preferred_element_type=jnp.float32)
    q_all = jnp.dot(lhs_sin, sin_tab, preferred_element_type=jnp.float32)
    r1, r2 = r_all[:rows], r_all[rows:]
    q1, q2 = q_all[:rows], q_all[rows:]

    def flux_of(grid_rows):
        return surface_flux(grid_rows.reshape(lat_dev, fields, levels, quarter), level_weight)

    strip0 = flux_of((r1 + q1)[:, :quarter])
    strip1 = jnp.flip(flux_of((r2 - q2)[:, 1 : quarter + 1]), axis=-1)
    strip2 = flux_of((r2 + q2)[:, :quarter])
    strip3 = jnp.flip(flux_of((r1 - q1)[:, 1 : quarter + 1]), axis=-1)
    partial_value = jnp.concatenate([strip0, strip1, strip2, strip3], axis=-1)

    own_first = (wave_at * cpl_count + cpl_at) * lat_dev
    source = lax.dynamic_slice_in_dim(source_row, own_first, lat_dev)
    weight_hi = lax.dynamic_slice_in_dim(row_weight, own_first, lat_dev)
    strip_width = NLON // lev_count
    by_strip = partial_value.reshape(lat_dev, fields, lev_count, strip_width).transpose(2, 0, 1, 3)
    summed = jnp.sum(
        lax.all_to_all(by_strip, "lev", split_axis=0, concat_axis=0, tiled=True), axis=0
    )
    copies = jnp.broadcast_to(summed[None], (wave_count * cpl_count,) + summed.shape)
    gathered = lax.all_to_all(copies, ("wave", "cpl"), split_axis=0, concat_axis=0, tiled=True)
    gathered = gathered.reshape((wave_count * cpl_count * lat_dev,) + summed.shape[1:])
    gathered = latitude_order(gathered, wave_count, cpl_count, lat_dev)
    return interpolate(gathered, source, weight_hi)


def solution(mesh):
    placed = (P("wave", None, None, "lev", None), P("wave", "cpl", None), P(), P("lev"), P(), P())
    return jax.shard_map(
        local,
        mesh=mesh,
        in_specs=placed,
        out_specs=P(("wave", "cpl"), None, "lev"),
        check_vma=False,
    )
```

```python
import math

import jax
import jax.numpy as jnp
from jax import lax
from jax.sharding import PartitionSpec as P
from jax.experimental import pallas as pl
from jax.experimental.pallas import tpu as pltpu

NLON = 4320
LANE = 128
SLOT_BLOCK = 64


def phase_angle(phase, lon_total):
    return phase.astype(jnp.float32) * (2.0 * math.pi / lon_total)


def surface_flux(grid_vals, level_weight):
    wind_speed = jnp.sqrt(grid_vals[:, 0] ** 2 + grid_vals[:, 1] ** 2 + 0.25)
    return jnp.sum(level_weight[:, None] * wind_speed[:, None] * grid_vals, axis=2)


def latitude_order(gathered, wave_count, cpl_count, lat_dev):
    trailing = gathered.shape[1:]
    gathered = gathered.reshape((wave_count, cpl_count, lat_dev) + trailing)
    gathered = jnp.swapaxes(gathered, 0, 1)
    return gathered.reshape((wave_count * cpl_count * lat_dev,) + trailing)


def interpolate(gathered, source, weight_hi):
    lower = jnp.take(gathered, source, axis=0)
    upper = jnp.take(gathered, source + 1, axis=0)
    return (1.0 - weight_hi[:, None, None]) * lower + weight_hi[:, None, None] * upper


def quarter_tables(wavenumber, width):
    blocks = width // LANE
    factor = jnp.where(wavenumber == 0, 1.0, 2.0).astype(jnp.float32)[:, None]
    offsets = jnp.arange(LANE, dtype=jnp.int32)
    base_angle = phase_angle(wavenumber[:, None] * offsets[None, :] % NLON, NLON)
    base_cos = jnp.cos(base_angle)[:, None, :]
    base_sin = jnp.sin(base_angle)[:, None, :]
    starts = jnp.arange(blocks, dtype=jnp.int32) * LANE
    start_angle = phase_angle(wavenumber[:, None] * starts[None, :] % NLON, NLON)
    start_cos = (factor * jnp.cos(start_angle))[:, :, None]
    start_sin = (factor * jnp.sin(start_angle))[:, :, None]
    cos_tab = start_cos * base_cos - start_sin * base_sin
    sin_tab = start_sin * base_cos + start_cos * base_sin
    slots = wavenumber.shape[0]
    return (
        cos_tab.astype(jnp.bfloat16).reshape(slots, width),
        (-sin_tab).astype(jnp.bfloat16).reshape(slots, width),
    )


def legendre_kernel(waves_ref, spec_ref, table_ref, out_ref):
    block = spec_ref.shape[0]
    degree = spec_ref.shape[-1]
    first = pl.program_id(0) * block

    def one_slot(s, carry):
        limit = degree - waves_ref[first + s]
        rows = table_ref[s]
        column = lax.broadcasted_iota(jnp.int32, rows.shape, 1)
        rows = jnp.where(column < limit, rows, jnp.zeros_like(rows))
        coefficient = spec_ref[s].reshape(-1, degree)
        out_ref[s] = lax.dot_general(
            rows, coefficient, (((1,), (1,)), ((), ())), preferred_element_type=jnp.float32
        ).astype(out_ref.dtype)
        return carry

    lax.fori_loop(0, block, one_slot, 0, unroll=True)


def legendre_transform(stored, legendre, owned_waves):
    slots, _, levels, fields, degree = stored.shape
    lats = legendre.shape[1]
    channels = 2 * levels * fields
    block = max(b for b in range(1, SLOT_BLOCK + 1) if slots % b == 0)
    return pl.pallas_call(
        legendre_kernel,
        out_shape=jax.ShapeDtypeStruct((slots, lats, channels), jnp.bfloat16),
        grid_spec=pltpu.PrefetchScalarGridSpec(
            num_scalar_prefetch=1,
            grid=(slots // block,),
            in_specs=[
                pl.BlockSpec((block, 2, levels, fields, degree), lambda i, w: (i, 0, 0, 0, 0)),
                pl.BlockSpec((block, lats, degree), lambda i, w: (i, 0, 0)),
            ],
            out_specs=pl.BlockSpec((block, lats, channels), lambda i, w: (i, 0, 0)),
        ),
        cost_estimate=pl.CostEstimate(
            flops=2 * slots * lats * channels * degree,
            bytes_accessed=2 * slots * degree * (channels + lats),
            transcendentals=0,
        ),
    )(owned_waves, stored, legendre)


def local(spectral, legendre, wavenumber, level_weight, source_row, row_weight):
    slot_count = spectral.shape[0]
    fields = spectral.shape[2]
    levels = spectral.shape[3]
    degree = spectral.shape[4]
    channels = 2 * fields * levels
    wave_count = lax.axis_size("wave")
    cpl_count = lax.axis_size("cpl")
    lev_count = lax.axis_size("lev")
    wave_at = lax.axis_index("wave")
    cpl_at = lax.axis_index("cpl")
    owned_waves = lax.dynamic_slice_in_dim(wavenumber, wave_at * slot_count, slot_count)
    stored = jnp.transpose(spectral, (0, 1, 3, 2, 4))
    spec_grid = (
        legendre_transform(stored, legendre, owned_waves)
        .reshape(slot_count, legendre.shape[1], 2, levels, fields)
        .transpose(0, 1, 2, 4, 3)
        .reshape(slot_count, legendre.shape[1], channels)
    )
    by_latitude = lax.all_to_all(spec_grid, "wave", split_axis=1, concat_axis=0, tiled=True)
    total_slots = by_latitude.shape[0]
    lat_dev = by_latitude.shape[1]
    rows = lat_dev * fields * levels
    parts = by_latitude.reshape(total_slots, lat_dev, 2, fields * levels)
    real = parts[:, :, 0].reshape(total_slots, rows).T
    imag = parts[:, :, 1].reshape(total_slots, rows).T
    parity = (1 - 2 * (wavenumber & 1)).astype(jnp.bfloat16)[None, :]
    lhs_cos = jnp.concatenate([real, real * parity], axis=0)
    lhs_sin = jnp.concatenate([imag, imag * parity], axis=0)

    quarter = NLON // 4
    width = -(-(quarter + 1) // LANE) * LANE
    cos_tab, sin_tab = quarter_tables(wavenumber, width)
    r_all = jnp.dot(lhs_cos, cos_tab, preferred_element_type=jnp.float32)
    q_all = jnp.dot(lhs_sin, sin_tab, preferred_element_type=jnp.float32)
    r1, r2 = r_all[:rows], r_all[rows:]
    q1, q2 = q_all[:rows], q_all[rows:]

    def flux_of(grid_rows):
        return surface_flux(grid_rows.reshape(lat_dev, fields, levels, quarter), level_weight)

    strip0 = flux_of((r1 + q1)[:, :quarter])
    strip1 = jnp.flip(flux_of((r2 - q2)[:, 1 : quarter + 1]), axis=-1)
    strip2 = flux_of((r2 + q2)[:, :quarter])
    strip3 = jnp.flip(flux_of((r1 - q1)[:, 1 : quarter + 1]), axis=-1)
    partial_value = jnp.concatenate([strip0, strip1, strip2, strip3], axis=-1)

    lat_total = wave_count * cpl_count * lat_dev
    row_at = lax.broadcasted_iota(jnp.int32, (source_row.shape[0], lat_total), 1)
    weights = jnp.where(row_at == source_row[:, None], (1.0 - row_weight)[:, None], 0.0) + jnp.where(
        row_at == source_row[:, None] + 1, row_weight[:, None], 0.0
    )
    own_rows = (cpl_at * wave_count + wave_at) * lat_dev
    own_weights = lax.dynamic_slice_in_dim(weights, own_rows, lat_dev, 1)
    own_weights = own_weights.reshape(wave_count, 1, cpl_count, lat_dev, lat_dev, 1, 1)
    strip_width = NLON // lev_count
    strips = partial_value.reshape(lat_dev, fields, lev_count, strip_width).transpose(2, 0, 1, 3)
    strips = strips.reshape(1, lev_count, 1, 1, lat_dev, fields, strip_width)
    shares = jnp.sum(own_weights * strips, axis=4)
    shares = shares.reshape((wave_count * lev_count * cpl_count, lat_dev, fields, strip_width))
    received = lax.all_to_all(shares, ("wave", "lev", "cpl"), split_axis=0, concat_axis=0, tiled=True)
    return jnp.sum(received, axis=0)


def solution(mesh):
    placed = (P("wave", None, None, "lev", None), P("wave", "cpl", None), P(), P("lev"), P(), P())
    return jax.shard_map(
        local,
        mesh=mesh,
        in_specs=placed,
        out_specs=P(("wave", "cpl"), None, "lev"),
        check_vma=False,
    )
```

```python
import math

import jax
import jax.numpy as jnp
from jax import lax
from jax.sharding import PartitionSpec as P
from jax.experimental import pallas as pl
from jax.experimental.pallas import tpu as pltpu

NLON = 4320
LANE = 128
SLOT_BLOCK = 64


def phase_angle(phase, lon_total):
    return phase.astype(jnp.float32) * (2.0 * math.pi / lon_total)


def surface_flux(grid_vals, level_weight):
    wind_speed = jnp.sqrt(grid_vals[:, 0] ** 2 + grid_vals[:, 1] ** 2 + 0.25)
    return jnp.sum(level_weight[:, None] * wind_speed[:, None] * grid_vals, axis=2)


def latitude_order(gathered, wave_count, cpl_count, lat_dev):
    trailing = gathered.shape[1:]
    gathered = gathered.reshape((wave_count, cpl_count, lat_dev) + trailing)
    gathered = jnp.swapaxes(gathered, 0, 1)
    return gathered.reshape((wave_count * cpl_count * lat_dev,) + trailing)


def interpolate(gathered, source, weight_hi):
    lower = jnp.take(gathered, source, axis=0)
    upper = jnp.take(gathered, source + 1, axis=0)
    return (1.0 - weight_hi[:, None, None]) * lower + weight_hi[:, None, None] * upper


def quarter_tables(wavenumber, width):
    blocks = width // LANE
    factor = jnp.where(wavenumber == 0, 1.0, 2.0).astype(jnp.float32)[:, None]
    offsets = jnp.arange(LANE, dtype=jnp.int32)
    base_angle = phase_angle(wavenumber[:, None] * offsets[None, :] % NLON, NLON)
    base_cos = jnp.cos(base_angle)[:, None, :]
    base_sin = jnp.sin(base_angle)[:, None, :]
    starts = jnp.arange(blocks, dtype=jnp.int32) * LANE
    start_angle = phase_angle(wavenumber[:, None] * starts[None, :] % NLON, NLON)
    start_cos = (factor * jnp.cos(start_angle))[:, :, None]
    start_sin = (factor * jnp.sin(start_angle))[:, :, None]
    cos_tab = start_cos * base_cos - start_sin * base_sin
    sin_tab = start_sin * base_cos + start_cos * base_sin
    slots = wavenumber.shape[0]
    return (
        cos_tab.astype(jnp.bfloat16).reshape(slots, width),
        (-sin_tab).astype(jnp.bfloat16).reshape(slots, width),
    )


def legendre_kernel(waves_ref, spec_ref, table_ref, out_ref):
    block = spec_ref.shape[0]
    degree = spec_ref.shape[-1]
    first = pl.program_id(0) * block

    def one_slot(s, carry):
        limit = degree - waves_ref[first + s]
        rows = table_ref[s]
        column = lax.broadcasted_iota(jnp.int32, rows.shape, 1)
        rows = jnp.where(column < limit, rows, jnp.zeros_like(rows))
        coefficient = spec_ref[s].reshape(-1, degree)
        out_ref[s] = lax.dot_general(
            rows, coefficient, (((1,), (1,)), ((), ())), preferred_element_type=jnp.float32
        ).astype(out_ref.dtype)
        return carry

    lax.fori_loop(0, block, one_slot, 0, unroll=True)


def legendre_transform(stored, legendre, owned_waves):
    slots, _, levels, fields, degree = stored.shape
    lats = legendre.shape[1]
    channels = 2 * levels * fields
    block = max(b for b in range(1, SLOT_BLOCK + 1) if slots % b == 0)
    return pl.pallas_call(
        legendre_kernel,
        out_shape=jax.ShapeDtypeStruct((slots, lats, channels), jnp.bfloat16),
        grid_spec=pltpu.PrefetchScalarGridSpec(
            num_scalar_prefetch=1,
            grid=(slots // block,),
            in_specs=[
                pl.BlockSpec((block, 2, levels, fields, degree), lambda i, w: (i, 0, 0, 0, 0)),
                pl.BlockSpec((block, lats, degree), lambda i, w: (i, 0, 0)),
            ],
            out_specs=pl.BlockSpec((block, lats, channels), lambda i, w: (i, 0, 0)),
        ),
        cost_estimate=pl.CostEstimate(
            flops=2 * slots * lats * channels * degree,
            bytes_accessed=2 * slots * degree * (channels + lats),
            transcendentals=0,
        ),
    )(owned_waves, stored, legendre)


def local(spectral, legendre, wavenumber, level_weight, source_row, row_weight):
    slot_count = spectral.shape[0]
    fields = spectral.shape[2]
    levels = spectral.shape[3]
    degree = spectral.shape[4]
    channels = 2 * fields * levels
    wave_count = lax.axis_size("wave")
    cpl_count = lax.axis_size("cpl")
    lev_count = lax.axis_size("lev")
    wave_at = lax.axis_index("wave")
    cpl_at = lax.axis_index("cpl")
    owned_waves = lax.dynamic_slice_in_dim(wavenumber, wave_at * slot_count, slot_count)
    stored = jnp.transpose(spectral, (0, 1, 3, 2, 4))
    spec_grid = (
        legendre_transform(stored, legendre, owned_waves)
        .reshape(slot_count, legendre.shape[1], 2, levels, fields)
        .transpose(0, 1, 2, 4, 3)
        .reshape(slot_count, legendre.shape[1], channels)
    )
    by_latitude = lax.all_to_all(spec_grid, "wave", split_axis=1, concat_axis=0, tiled=True)
    total_slots = by_latitude.shape[0]
    lat_dev = by_latitude.shape[1]
    rows = lat_dev * fields * levels
    parts = by_latitude.reshape(total_slots, lat_dev, 2, fields * levels)
    real = parts[:, :, 0].reshape(total_slots, rows).T
    imag = parts[:, :, 1].reshape(total_slots, rows).T
    parity = (1 - 2 * (wavenumber & 1)).astype(jnp.bfloat16)[None, :]
    lhs_cos = jnp.concatenate([real, real * parity], axis=0)
    lhs_sin = jnp.concatenate([imag, imag * parity], axis=0)

    quarter = NLON // 4
    width = -(-(quarter + 1) // LANE) * LANE
    cos_tab, sin_tab = quarter_tables(wavenumber, width)
    r_all = jnp.dot(lhs_cos, cos_tab, preferred_element_type=jnp.float32)
    q_all = jnp.dot(lhs_sin, sin_tab, preferred_element_type=jnp.float32)
    r1, r2 = r_all[:rows], r_all[rows:]
    q1, q2 = q_all[:rows], q_all[rows:]

    def flux_of(grid_rows):
        return surface_flux(grid_rows.reshape(lat_dev, fields, levels, quarter), level_weight)

    strip0 = flux_of((r1 + q1)[:, :quarter])
    strip1 = jnp.flip(flux_of((r2 - q2)[:, 1 : quarter + 1]), axis=-1)
    strip2 = flux_of((r2 + q2)[:, :quarter])
    strip3 = jnp.flip(flux_of((r1 - q1)[:, 1 : quarter + 1]), axis=-1)
    partial_value = jnp.concatenate([strip0, strip1, strip2, strip3], axis=-1)

    own_first = (wave_at * cpl_count + cpl_at) * lat_dev
    source = lax.dynamic_slice_in_dim(source_row, own_first, lat_dev)
    weight_hi = lax.dynamic_slice_in_dim(row_weight, own_first, lat_dev)
    strip_width = NLON // lev_count
    lev_at = lax.axis_index("lev")
    by_strip = partial_value.reshape(lat_dev, fields, lev_count, strip_width).transpose(2, 0, 1, 3)
    summed = lax.dynamic_index_in_dim(by_strip, lev_at, 0, keepdims=False)
    for k in range(1, lev_count):
        outgoing = lax.dynamic_index_in_dim(by_strip, (lev_at + k) % lev_count, 0, keepdims=False)
        pairs = [(j, (j + k) % lev_count) for j in range(lev_count)]
        summed = summed + lax.ppermute(outgoing, "lev", pairs)
    group = wave_count * cpl_count
    own = wave_at * cpl_count + cpl_at
    arrived = [summed]
    for k in range(1, group):
        pairs = [(j, (j + k) % group) for j in range(group)]
        arrived.append(lax.ppermute(summed, ("wave", "cpl"), pairs))
    stacked = jnp.stack(arrived)
    member = (own - jnp.arange(group, dtype=jnp.int32)) % group
    gathered = jnp.take(stacked, member, axis=0)
    gathered = gathered.reshape((group * lat_dev,) + summed.shape[1:])
    gathered = latitude_order(gathered, wave_count, cpl_count, lat_dev)
    return interpolate(gathered, source, weight_hi)


def solution(mesh):
    placed = (P("wave", None, None, "lev", None), P("wave", "cpl", None), P(), P("lev"), P(), P())
    return jax.shard_map(
        local,
        mesh=mesh,
        in_specs=placed,
        out_specs=P(("wave", "cpl"), None, "lev"),
        check_vma=False,
    )
```

```python
import math

import jax
import jax.numpy as jnp
from jax import lax
from jax.sharding import PartitionSpec as P
from jax.experimental import pallas as pl
from jax.experimental.pallas import tpu as pltpu

NLON = 4320
LANE = 128
SLOT_BLOCK = 64


def phase_angle(phase, lon_total):
    return phase.astype(jnp.float32) * (2.0 * math.pi / lon_total)


def surface_flux(grid_vals, level_weight):
    wind_speed = jnp.sqrt(grid_vals[:, 0] ** 2 + grid_vals[:, 1] ** 2 + 0.25)
    return jnp.sum(level_weight[:, None] * wind_speed[:, None] * grid_vals, axis=2)


def latitude_order(gathered, wave_count, cpl_count, lat_dev):
    trailing = gathered.shape[1:]
    gathered = gathered.reshape((wave_count, cpl_count, lat_dev) + trailing)
    gathered = jnp.swapaxes(gathered, 0, 1)
    return gathered.reshape((wave_count * cpl_count * lat_dev,) + trailing)


def interpolate(gathered, source, weight_hi):
    lower = jnp.take(gathered, source, axis=0)
    upper = jnp.take(gathered, source + 1, axis=0)
    return (1.0 - weight_hi[:, None, None]) * lower + weight_hi[:, None, None] * upper


def quarter_tables(wavenumber, width):
    blocks = width // LANE
    factor = jnp.where(wavenumber == 0, 1.0, 2.0).astype(jnp.float32)[:, None]
    offsets = jnp.arange(LANE, dtype=jnp.int32)
    base_angle = phase_angle(wavenumber[:, None] * offsets[None, :] % NLON, NLON)
    base_cos = jnp.cos(base_angle)[:, None, :]
    base_sin = jnp.sin(base_angle)[:, None, :]
    starts = jnp.arange(blocks, dtype=jnp.int32) * LANE
    start_angle = phase_angle(wavenumber[:, None] * starts[None, :] % NLON, NLON)
    start_cos = (factor * jnp.cos(start_angle))[:, :, None]
    start_sin = (factor * jnp.sin(start_angle))[:, :, None]
    cos_tab = start_cos * base_cos - start_sin * base_sin
    sin_tab = start_sin * base_cos + start_cos * base_sin
    slots = wavenumber.shape[0]
    return (
        cos_tab.astype(jnp.bfloat16).reshape(slots, width),
        (-sin_tab).astype(jnp.bfloat16).reshape(slots, width),
    )


def legendre_kernel(waves_ref, spec_hbm, table_ref, out_ref, buf, sem):
    block = out_ref.shape[0]
    degree = table_ref.shape[-1]
    chunk = 256 if degree % 256 == 0 else LANE
    chunks = degree // chunk
    step = pl.program_id(0)
    steps = pl.num_programs(0)

    def each_copy(at, held, act):
        def one(s, carry):
            needed = (degree - waves_ref[at * block + s] + chunk - 1) // chunk
            for n in range(1, chunks + 1):

                @pl.when(needed == n)
                def _():
                    act(
                        pltpu.make_async_copy(
                            spec_hbm.at[at * block + s, :, :, :, pl.ds(0, n * chunk)],
                            buf.at[held, s, :, :, :, pl.ds(0, n * chunk)],
                            sem.at[held],
                        )
                    )

            return carry

        lax.fori_loop(0, block, one, 0)

    @pl.when(step == 0)
    def _():
        each_copy(0, 0, lambda c: c.start())

    @pl.when(step + 1 < steps)
    def _():
        each_copy(step + 1, (step + 1) % 2, lambda c: c.start())

    current = step % 2
    each_copy(step, current, lambda c: c.wait())
    first = step * block

    def one_slot(s, carry):
        limit = degree - waves_ref[first + s]
        coefficient = buf[current, s].reshape(-1, degree).astype(jnp.float32)
        column = lax.broadcasted_iota(jnp.int32, coefficient.shape, 1)
        coefficient = jnp.where(column < limit, coefficient, 0.0).astype(jnp.bfloat16)
        out_ref[s] = lax.dot_general(
            table_ref[s], coefficient, (((1,), (1,)), ((), ())), preferred_element_type=jnp.float32
        ).astype(out_ref.dtype)
        return carry

    lax.fori_loop(0, block, one_slot, 0, unroll=True)


def legendre_transform(stored, legendre, owned_waves):
    slots, _, levels, fields, degree = stored.shape
    lats = legendre.shape[1]
    channels = 2 * levels * fields
    block = max(b for b in range(1, SLOT_BLOCK + 1) if slots % b == 0)
    return pl.pallas_call(
        legendre_kernel,
        out_shape=jax.ShapeDtypeStruct((slots, lats, channels), jnp.bfloat16),
        grid_spec=pltpu.PrefetchScalarGridSpec(
            num_scalar_prefetch=1,
            grid=(slots // block,),
            in_specs=[
                pl.BlockSpec(memory_space=pl.ANY),
                pl.BlockSpec((block, lats, degree), lambda i, w: (i, 0, 0)),
            ],
            out_specs=pl.BlockSpec((block, lats, channels), lambda i, w: (i, 0, 0)),
            scratch_shapes=[
                pltpu.VMEM((2, block, 2, levels, fields, degree), stored.dtype),
                pltpu.SemaphoreType.DMA((2,)),
            ],
        ),
        cost_estimate=pl.CostEstimate(
            flops=2 * slots * lats * channels * degree,
            bytes_accessed=slots * degree * (channels + lats),
            transcendentals=0,
        ),
    )(owned_waves, stored, legendre)


def local(spectral, legendre, wavenumber, level_weight, source_row, row_weight):
    slot_count = spectral.shape[0]
    fields = spectral.shape[2]
    levels = spectral.shape[3]
    degree = spectral.shape[4]
    channels = 2 * fields * levels
    wave_count = lax.axis_size("wave")
    cpl_count = lax.axis_size("cpl")
    lev_count = lax.axis_size("lev")
    wave_at = lax.axis_index("wave")
    cpl_at = lax.axis_index("cpl")
    owned_waves = lax.dynamic_slice_in_dim(wavenumber, wave_at * slot_count, slot_count)
    stored = jnp.transpose(spectral, (0, 1, 3, 2, 4))
    spec_grid = (
        legendre_transform(stored, legendre, owned_waves)
        .reshape(slot_count, legendre.shape[1], 2, levels, fields)
        .transpose(0, 1, 2, 4, 3)
        .reshape(slot_count, legendre.shape[1], channels)
    )
    by_latitude = lax.all_to_all(spec_grid, "wave", split_axis=1, concat_axis=0, tiled=True)
    total_slots = by_latitude.shape[0]
    lat_dev = by_latitude.shape[1]
    rows = lat_dev * fields * levels
    parts = by_latitude.reshape(total_slots, lat_dev, 2, fields * levels)
    real = parts[:, :, 0].reshape(total_slots, rows).T
    imag = parts[:, :, 1].reshape(total_slots, rows).T
    parity = (1 - 2 * (wavenumber & 1)).astype(jnp.bfloat16)[None, :]
    lhs_cos = jnp.concatenate([real, real * parity], axis=0)
    lhs_sin = jnp.concatenate([imag, imag * parity], axis=0)

    quarter = NLON // 4
    width = -(-(quarter + 1) // LANE) * LANE
    cos_tab, sin_tab = quarter_tables(wavenumber, width)
    r_all = jnp.dot(lhs_cos, cos_tab, preferred_element_type=jnp.float32)
    q_all = jnp.dot(lhs_sin, sin_tab, preferred_element_type=jnp.float32)
    r1, r2 = r_all[:rows], r_all[rows:]
    q1, q2 = q_all[:rows], q_all[rows:]

    def flux_of(grid_rows):
        return surface_flux(grid_rows.reshape(lat_dev, fields, levels, quarter), level_weight)

    strip0 = flux_of((r1 + q1)[:, :quarter])
    strip1 = jnp.flip(flux_of((r2 - q2)[:, 1 : quarter + 1]), axis=-1)
    strip2 = flux_of((r2 + q2)[:, :quarter])
    strip3 = jnp.flip(flux_of((r1 - q1)[:, 1 : quarter + 1]), axis=-1)
    partial_value = jnp.concatenate([strip0, strip1, strip2, strip3], axis=-1)

    own_first = (wave_at * cpl_count + cpl_at) * lat_dev
    source = lax.dynamic_slice_in_dim(source_row, own_first, lat_dev)
    weight_hi = lax.dynamic_slice_in_dim(row_weight, own_first, lat_dev)
    strip_width = NLON // lev_count
    by_strip = partial_value.reshape(lat_dev, fields, lev_count, strip_width).transpose(2, 0, 1, 3)
    summed = jnp.sum(
        lax.all_to_all(by_strip, "lev", split_axis=0, concat_axis=0, tiled=True), axis=0
    )
    copies = jnp.broadcast_to(summed[None], (wave_count * cpl_count,) + summed.shape)
    gathered = lax.all_to_all(copies, ("wave", "cpl"), split_axis=0, concat_axis=0, tiled=True)
    gathered = gathered.reshape((wave_count * cpl_count * lat_dev,) + summed.shape[1:])
    gathered = latitude_order(gathered, wave_count, cpl_count, lat_dev)
    return interpolate(gathered, source, weight_hi)


def solution(mesh):
    placed = (P("wave", None, None, "lev", None), P("wave", "cpl", None), P(), P("lev"), P(), P())
    return jax.shard_map(
        local,
        mesh=mesh,
        in_specs=placed,
        out_specs=P(("wave", "cpl"), None, "lev"),
        check_vma=False,
    )
```

```python
import math

import jax
import jax.numpy as jnp
from jax import lax
from jax.sharding import PartitionSpec as P
from jax.experimental import pallas as pl
from jax.experimental.pallas import tpu as pltpu

NLON = 4320
LANE = 128
SLOT_BLOCK = 64


def phase_angle(phase, lon_total):
    return phase.astype(jnp.float32) * (2.0 * math.pi / lon_total)


def surface_flux(grid_vals, level_weight):
    wind_speed = jnp.sqrt(grid_vals[:, 0] ** 2 + grid_vals[:, 1] ** 2 + 0.25)
    return jnp.sum(level_weight[:, None] * wind_speed[:, None] * grid_vals, axis=2)


def latitude_order(gathered, wave_count, cpl_count, lat_dev):
    trailing = gathered.shape[1:]
    gathered = gathered.reshape((wave_count, cpl_count, lat_dev) + trailing)
    gathered = jnp.swapaxes(gathered, 0, 1)
    return gathered.reshape((wave_count * cpl_count * lat_dev,) + trailing)


def interpolate(gathered, source, weight_hi):
    lower = jnp.take(gathered, source, axis=0)
    upper = jnp.take(gathered, source + 1, axis=0)
    return (1.0 - weight_hi[:, None, None]) * lower + weight_hi[:, None, None] * upper


def quarter_tables(wavenumber, width):
    blocks = width // LANE
    factor = jnp.where(wavenumber == 0, 1.0, 2.0).astype(jnp.float32)[:, None]
    offsets = jnp.arange(LANE, dtype=jnp.int32)
    base_angle = phase_angle(wavenumber[:, None] * offsets[None, :] % NLON, NLON)
    base_cos = jnp.cos(base_angle)[:, None, :]
    base_sin = jnp.sin(base_angle)[:, None, :]
    starts = jnp.arange(blocks, dtype=jnp.int32) * LANE
    start_angle = phase_angle(wavenumber[:, None] * starts[None, :] % NLON, NLON)
    start_cos = (factor * jnp.cos(start_angle))[:, :, None]
    start_sin = (factor * jnp.sin(start_angle))[:, :, None]
    cos_tab = start_cos * base_cos - start_sin * base_sin
    sin_tab = start_sin * base_cos + start_cos * base_sin
    slots = wavenumber.shape[0]
    return (
        cos_tab.astype(jnp.bfloat16).reshape(slots, width),
        (-sin_tab).astype(jnp.bfloat16).reshape(slots, width),
    )


def legendre_kernel(waves_ref, spec_hbm, table_ref, out_ref, buf, sem):
    block = out_ref.shape[0]
    degree = table_ref.shape[-1]
    chunk = 256 if degree % 256 == 0 else LANE
    chunks = degree // chunk
    step = pl.program_id(0)
    steps = pl.num_programs(0)

    def each_copy(at, held, act):
        def one(s, carry):
            needed = (degree - waves_ref[at * block + s] + chunk - 1) // chunk
            for n in range(1, chunks + 1):

                @pl.when(needed == n)
                def _():
                    act(
                        pltpu.make_async_copy(
                            spec_hbm.at[at * block + s, :, :, :, pl.ds(0, n * chunk)],
                            buf.at[held, s, :, :, :, pl.ds(0, n * chunk)],
                            sem.at[held],
                        )
                    )

            return carry

        lax.fori_loop(0, block, one, 0)

    @pl.when(step == 0)
    def _():
        buf[...] = jnp.zeros(buf.shape, buf.dtype)
        each_copy(0, 0, lambda c: c.start())

    @pl.when(step + 1 < steps)
    def _():
        each_copy(step + 1, (step + 1) % 2, lambda c: c.start())

    current = step % 2
    each_copy(step, current, lambda c: c.wait())
    first = step * block

    def one_slot(s, carry):
        limit = degree - waves_ref[first + s]
        coefficient = buf[current, s].reshape(-1, degree)
        rows = table_ref[s]
        column = lax.broadcasted_iota(jnp.int32, rows.shape, 1)
        rows = jnp.where(column < limit, rows, jnp.zeros_like(rows))
        out_ref[s] = lax.dot_general(
            rows, coefficient, (((1,), (1,)), ((), ())), preferred_element_type=jnp.float32
        ).astype(out_ref.dtype)
        return carry

    lax.fori_loop(0, block, one_slot, 0, unroll=True)


def legendre_transform(stored, legendre, owned_waves):
    slots, _, levels, fields, degree = stored.shape
    lats = legendre.shape[1]
    channels = 2 * levels * fields
    block = max(b for b in range(1, SLOT_BLOCK + 1) if slots % b == 0)
    return pl.pallas_call(
        legendre_kernel,
        out_shape=jax.ShapeDtypeStruct((slots, lats, channels), jnp.bfloat16),
        grid_spec=pltpu.PrefetchScalarGridSpec(
            num_scalar_prefetch=1,
            grid=(slots // block,),
            in_specs=[
                pl.BlockSpec(memory_space=pl.ANY),
                pl.BlockSpec((block, lats, degree), lambda i, w: (i, 0, 0)),
            ],
            out_specs=pl.BlockSpec((block, lats, channels), lambda i, w: (i, 0, 0)),
            scratch_shapes=[
                pltpu.VMEM((2, block, 2, levels, fields, degree), stored.dtype),
                pltpu.SemaphoreType.DMA((2,)),
            ],
        ),
        cost_estimate=pl.CostEstimate(
            flops=2 * slots * lats * channels * degree,
            bytes_accessed=slots * degree * (channels + lats),
            transcendentals=0,
        ),
    )(owned_waves, stored, legendre)


def local(spectral, legendre, wavenumber, level_weight, source_row, row_weight):
    slot_count = spectral.shape[0]
    fields = spectral.shape[2]
    levels = spectral.shape[3]
    degree = spectral.shape[4]
    channels = 2 * fields * levels
    wave_count = lax.axis_size("wave")
    cpl_count = lax.axis_size("cpl")
    lev_count = lax.axis_size("lev")
    wave_at = lax.axis_index("wave")
    cpl_at = lax.axis_index("cpl")
    owned_waves = lax.dynamic_slice_in_dim(wavenumber, wave_at * slot_count, slot_count)
    stored = jnp.transpose(spectral, (0, 1, 3, 2, 4))
    spec_grid = (
        legendre_transform(stored, legendre, owned_waves)
        .reshape(slot_count, legendre.shape[1], 2, levels, fields)
        .transpose(0, 1, 2, 4, 3)
        .reshape(slot_count, legendre.shape[1], channels)
    )
    by_latitude = lax.all_to_all(spec_grid, "wave", split_axis=1, concat_axis=0, tiled=True)
    total_slots = by_latitude.shape[0]
    lat_dev = by_latitude.shape[1]
    rows = lat_dev * fields * levels
    parts = by_latitude.reshape(total_slots, lat_dev, 2, fields * levels)
    real = parts[:, :, 0].reshape(total_slots, rows).T
    imag = parts[:, :, 1].reshape(total_slots, rows).T
    parity = (1 - 2 * (wavenumber & 1)).astype(jnp.bfloat16)[None, :]
    lhs_cos = jnp.concatenate([real, real * parity], axis=0)
    lhs_sin = jnp.concatenate([imag, imag * parity], axis=0)

    quarter = NLON // 4
    width = -(-(quarter + 1) // LANE) * LANE
    cos_tab, sin_tab = quarter_tables(wavenumber, width)
    r_all = jnp.dot(lhs_cos, cos_tab, preferred_element_type=jnp.float32)
    q_all = jnp.dot(lhs_sin, sin_tab, preferred_element_type=jnp.float32)
    r1, r2 = r_all[:rows], r_all[rows:]
    q1, q2 = q_all[:rows], q_all[rows:]

    def flux_of(grid_rows):
        return surface_flux(grid_rows.reshape(lat_dev, fields, levels, quarter), level_weight)

    strip0 = flux_of((r1 + q1)[:, :quarter])
    strip1 = jnp.flip(flux_of((r2 - q2)[:, 1 : quarter + 1]), axis=-1)
    strip2 = flux_of((r2 + q2)[:, :quarter])
    strip3 = jnp.flip(flux_of((r1 - q1)[:, 1 : quarter + 1]), axis=-1)
    partial_value = jnp.concatenate([strip0, strip1, strip2, strip3], axis=-1)

    own_first = (wave_at * cpl_count + cpl_at) * lat_dev
    source = lax.dynamic_slice_in_dim(source_row, own_first, lat_dev)
    weight_hi = lax.dynamic_slice_in_dim(row_weight, own_first, lat_dev)
    strip_width = NLON // lev_count
    by_strip = partial_value.reshape(lat_dev, fields, lev_count, strip_width).transpose(2, 0, 1, 3)
    summed = jnp.sum(
        lax.all_to_all(by_strip, "lev", split_axis=0, concat_axis=0, tiled=True), axis=0
    )
    copies = jnp.broadcast_to(summed[None], (wave_count * cpl_count,) + summed.shape)
    gathered = lax.all_to_all(copies, ("wave", "cpl"), split_axis=0, concat_axis=0, tiled=True)
    gathered = gathered.reshape((wave_count * cpl_count * lat_dev,) + summed.shape[1:])
    gathered = latitude_order(gathered, wave_count, cpl_count, lat_dev)
    return interpolate(gathered, source, weight_hi)


def solution(mesh):
    placed = (P("wave", None, None, "lev", None), P("wave", "cpl", None), P(), P("lev"), P(), P())
    return jax.shard_map(
        local,
        mesh=mesh,
        in_specs=placed,
        out_specs=P(("wave", "cpl"), None, "lev"),
        check_vma=False,
    )
```

```python
import math

import jax
import jax.numpy as jnp
from jax import lax
from jax.sharding import PartitionSpec as P
from jax.experimental import pallas as pl
from jax.experimental.pallas import tpu as pltpu

NLON = 4320
LANE = 128
SLOT_BLOCK = 64


def phase_angle(phase, lon_total):
    return phase.astype(jnp.float32) * (2.0 * math.pi / lon_total)


def surface_flux(grid_vals, level_weight):
    wind_speed = jnp.sqrt(grid_vals[:, 0] ** 2 + grid_vals[:, 1] ** 2 + 0.25)
    return jnp.sum(level_weight[:, None] * wind_speed[:, None] * grid_vals, axis=2)


def latitude_order(gathered, wave_count, cpl_count, lat_dev):
    trailing = gathered.shape[1:]
    gathered = gathered.reshape((wave_count, cpl_count, lat_dev) + trailing)
    gathered = jnp.swapaxes(gathered, 0, 1)
    return gathered.reshape((wave_count * cpl_count * lat_dev,) + trailing)


def interpolate(gathered, source, weight_hi):
    lower = jnp.take(gathered, source, axis=0)
    upper = jnp.take(gathered, source + 1, axis=0)
    return (1.0 - weight_hi[:, None, None]) * lower + weight_hi[:, None, None] * upper


def quarter_tables(wavenumber, width):
    blocks = width // LANE
    factor = jnp.where(wavenumber == 0, 1.0, 2.0).astype(jnp.float32)[:, None]
    fine_count = 16
    fine = jnp.arange(fine_count, dtype=jnp.int32)
    coarse = jnp.arange(LANE // fine_count, dtype=jnp.int32) * fine_count
    fine_angle = phase_angle(wavenumber[:, None] * fine[None, :] % NLON, NLON)[:, None, :]
    coarse_angle = phase_angle(wavenumber[:, None] * coarse[None, :] % NLON, NLON)[:, :, None]
    fine_cos, fine_sin = jnp.cos(fine_angle), jnp.sin(fine_angle)
    coarse_cos, coarse_sin = jnp.cos(coarse_angle), jnp.sin(coarse_angle)
    base_cos = (coarse_cos * fine_cos - coarse_sin * fine_sin).reshape(-1, 1, LANE)
    base_sin = (coarse_sin * fine_cos + coarse_cos * fine_sin).reshape(-1, 1, LANE)
    starts = jnp.arange(blocks, dtype=jnp.int32) * LANE
    start_angle = phase_angle(wavenumber[:, None] * starts[None, :] % NLON, NLON)
    start_cos = (factor * jnp.cos(start_angle))[:, :, None]
    start_sin = (factor * jnp.sin(start_angle))[:, :, None]
    cos_tab = start_cos * base_cos - start_sin * base_sin
    sin_tab = start_sin * base_cos + start_cos * base_sin
    slots = wavenumber.shape[0]
    return (
        cos_tab.astype(jnp.bfloat16).reshape(slots, width),
        (-sin_tab).astype(jnp.bfloat16).reshape(slots, width),
    )


def legendre_kernel(offset_ref, waves_ref, spec_ref, table_ref, out_ref):
    block = spec_ref.shape[0]
    degree = spec_ref.shape[-1]
    first = offset_ref[0] + pl.program_id(0) * block

    def one_slot(s, carry):
        limit = degree - waves_ref[first + s]
        rows = table_ref[s]
        column = lax.broadcasted_iota(jnp.int32, rows.shape, 1)
        rows = jnp.where(column < limit, rows, jnp.zeros_like(rows))
        coefficient = spec_ref[s].reshape(-1, degree)
        out_ref[s] = lax.dot_general(
            rows, coefficient, (((1,), (1,)), ((), ())), preferred_element_type=jnp.float32
        ).astype(out_ref.dtype)
        return carry

    lax.fori_loop(0, block, one_slot, 0, unroll=True)


def legendre_transform(stored, legendre, wavenumber, offset):
    slots, _, levels, fields, degree = stored.shape
    lats = legendre.shape[1]
    channels = 2 * levels * fields
    block = max(b for b in range(1, SLOT_BLOCK + 1) if slots % b == 0)
    return pl.pallas_call(
        legendre_kernel,
        out_shape=jax.ShapeDtypeStruct((slots, lats, channels), jnp.bfloat16),
        grid_spec=pltpu.PrefetchScalarGridSpec(
            num_scalar_prefetch=2,
            grid=(slots // block,),
            in_specs=[
                pl.BlockSpec((block, 2, levels, fields, degree), lambda i, o, w: (i, 0, 0, 0, 0)),
                pl.BlockSpec((block, lats, degree), lambda i, o, w: (i, 0, 0)),
            ],
            out_specs=pl.BlockSpec((block, lats, channels), lambda i, o, w: (i, 0, 0)),
        ),
        cost_estimate=pl.CostEstimate(
            flops=2 * slots * lats * channels * degree,
            bytes_accessed=2 * slots * degree * (channels + lats),
            transcendentals=0,
        ),
    )(offset, wavenumber, stored, legendre)


def local(spectral, legendre, wavenumber, level_weight, source_row, row_weight):
    slot_count = spectral.shape[0]
    fields = spectral.shape[2]
    levels = spectral.shape[3]
    degree = spectral.shape[4]
    channels = 2 * fields * levels
    wave_count = lax.axis_size("wave")
    cpl_count = lax.axis_size("cpl")
    lev_count = lax.axis_size("lev")
    wave_at = lax.axis_index("wave")
    cpl_at = lax.axis_index("cpl")
    stored = jnp.transpose(spectral, (0, 1, 3, 2, 4))
    spec_grid = (
        legendre_transform(
            stored, legendre, wavenumber, (wave_at * slot_count).astype(jnp.int32).reshape(1)
        )
        .reshape(slot_count, legendre.shape[1], 2, levels, fields)
        .transpose(0, 1, 2, 4, 3)
        .reshape(slot_count, legendre.shape[1], channels)
    )
    by_latitude = lax.all_to_all(spec_grid, "wave", split_axis=1, concat_axis=0, tiled=True)
    total_slots = by_latitude.shape[0]
    lat_dev = by_latitude.shape[1]
    rows = lat_dev * fields * levels
    parts = by_latitude.reshape(total_slots, lat_dev, 2, fields * levels)
    real = parts[:, :, 0].reshape(total_slots, rows).T
    imag = parts[:, :, 1].reshape(total_slots, rows).T
    parity = (1 - 2 * (wavenumber & 1)).astype(jnp.bfloat16)[None, :]
    lhs_cos = jnp.concatenate([real, real * parity], axis=0)
    lhs_sin = jnp.concatenate([imag, imag * parity], axis=0)

    quarter = NLON // 4
    width = -(-(quarter + 1) // LANE) * LANE
    cos_tab, sin_tab = quarter_tables(wavenumber, width)
    r_all = jnp.dot(lhs_cos, cos_tab, preferred_element_type=jnp.float32)
    q_all = jnp.dot(lhs_sin, sin_tab, preferred_element_type=jnp.float32)
    r1, r2 = r_all[:rows], r_all[rows:]
    q1, q2 = q_all[:rows], q_all[rows:]

    def flux_of(grid_rows):
        return surface_flux(grid_rows.reshape(lat_dev, fields, levels, quarter), level_weight)

    strip0 = flux_of((r1 + q1)[:, :quarter])
    strip1 = jnp.flip(flux_of((r2 - q2)[:, 1 : quarter + 1]), axis=-1)
    strip2 = flux_of((r2 + q2)[:, :quarter])
    strip3 = jnp.flip(flux_of((r1 - q1)[:, 1 : quarter + 1]), axis=-1)
    partial_value = jnp.concatenate([strip0, strip1, strip2, strip3], axis=-1)

    own_first = (wave_at * cpl_count + cpl_at) * lat_dev
    source = lax.dynamic_slice_in_dim(source_row, own_first, lat_dev)
    weight_hi = lax.dynamic_slice_in_dim(row_weight, own_first, lat_dev)
    strip_width = NLON // lev_count
    by_strip = partial_value.reshape(lat_dev, fields, lev_count, strip_width).transpose(2, 0, 1, 3)
    summed = jnp.sum(
        lax.all_to_all(by_strip, "lev", split_axis=0, concat_axis=0, tiled=True), axis=0
    )
    copies = jnp.broadcast_to(summed[None], (wave_count * cpl_count,) + summed.shape)
    gathered = lax.all_to_all(copies, ("wave", "cpl"), split_axis=0, concat_axis=0, tiled=True)
    gathered = gathered.reshape((wave_count * cpl_count * lat_dev,) + summed.shape[1:])
    gathered = latitude_order(gathered, wave_count, cpl_count, lat_dev)
    return interpolate(gathered, source, weight_hi)


def solution(mesh):
    placed = (P("wave", None, None, "lev", None), P("wave", "cpl", None), P(), P("lev"), P(), P())
    return jax.shard_map(
        local,
        mesh=mesh,
        in_specs=placed,
        out_specs=P(("wave", "cpl"), None, "lev"),
        check_vma=False,
    )
```

```python
import math

import jax
import jax.numpy as jnp
from jax import lax
from jax.sharding import PartitionSpec as P
from jax.experimental import pallas as pl
from jax.experimental.pallas import tpu as pltpu

NLON = 4320
LANE = 128
SLOT_BLOCK = 64


def phase_angle(phase, lon_total):
    return phase.astype(jnp.float32) * (2.0 * math.pi / lon_total)


def surface_flux(grid_vals, level_weight):
    wind_speed = jnp.sqrt(grid_vals[:, :, 0] ** 2 + grid_vals[:, :, 1] ** 2 + 0.25)
    return jnp.sum(level_weight[:, None, None] * wind_speed[:, :, None] * grid_vals, axis=1)


def latitude_order(gathered, wave_count, cpl_count, lat_dev):
    trailing = gathered.shape[1:]
    gathered = gathered.reshape((wave_count, cpl_count, lat_dev) + trailing)
    gathered = jnp.swapaxes(gathered, 0, 1)
    return gathered.reshape((wave_count * cpl_count * lat_dev,) + trailing)


def interpolate(gathered, source, weight_hi):
    lower = jnp.take(gathered, source, axis=0)
    upper = jnp.take(gathered, source + 1, axis=0)
    return (1.0 - weight_hi[:, None, None]) * lower + weight_hi[:, None, None] * upper


def quarter_tables(wavenumber, width):
    blocks = width // LANE
    factor = jnp.where(wavenumber == 0, 1.0, 2.0).astype(jnp.float32)[:, None]
    fine_count = 16
    fine = jnp.arange(fine_count, dtype=jnp.int32)
    coarse = jnp.arange(LANE // fine_count, dtype=jnp.int32) * fine_count
    fine_angle = phase_angle(wavenumber[:, None] * fine[None, :] % NLON, NLON)[:, None, :]
    coarse_angle = phase_angle(wavenumber[:, None] * coarse[None, :] % NLON, NLON)[:, :, None]
    fine_cos, fine_sin = jnp.cos(fine_angle), jnp.sin(fine_angle)
    coarse_cos, coarse_sin = jnp.cos(coarse_angle), jnp.sin(coarse_angle)
    base_cos = (coarse_cos * fine_cos - coarse_sin * fine_sin).reshape(-1, 1, LANE)
    base_sin = (coarse_sin * fine_cos + coarse_cos * fine_sin).reshape(-1, 1, LANE)
    starts = jnp.arange(blocks, dtype=jnp.int32) * LANE
    start_angle = phase_angle(wavenumber[:, None] * starts[None, :] % NLON, NLON)
    start_cos = (factor * jnp.cos(start_angle))[:, :, None]
    start_sin = (factor * jnp.sin(start_angle))[:, :, None]
    cos_tab = start_cos * base_cos - start_sin * base_sin
    sin_tab = start_sin * base_cos + start_cos * base_sin
    slots = wavenumber.shape[0]
    return (
        cos_tab.astype(jnp.bfloat16).reshape(slots, width),
        (-sin_tab).astype(jnp.bfloat16).reshape(slots, width),
    )


def legendre_kernel(offset_ref, waves_ref, spec_ref, table_ref, out_ref):
    block = spec_ref.shape[0]
    degree = spec_ref.shape[-1]
    first = offset_ref[0] + pl.program_id(0) * block

    def one_slot(s, carry):
        limit = degree - waves_ref[first + s]
        rows = table_ref[s]
        column = lax.broadcasted_iota(jnp.int32, rows.shape, 1)
        rows = jnp.where(column < limit, rows, jnp.zeros_like(rows))
        coefficient = spec_ref[s].reshape(-1, degree)
        out_ref[s] = lax.dot_general(
            rows, coefficient, (((1,), (1,)), ((), ())), preferred_element_type=jnp.float32
        ).astype(out_ref.dtype)
        return carry

    lax.fori_loop(0, block, one_slot, 0, unroll=True)


def legendre_transform(stored, legendre, wavenumber, offset):
    slots, _, levels, fields, degree = stored.shape
    lats = legendre.shape[1]
    channels = 2 * levels * fields
    block = max(b for b in range(1, SLOT_BLOCK + 1) if slots % b == 0)
    return pl.pallas_call(
        legendre_kernel,
        out_shape=jax.ShapeDtypeStruct((slots, lats, channels), jnp.bfloat16),
        grid_spec=pltpu.PrefetchScalarGridSpec(
            num_scalar_prefetch=2,
            grid=(slots // block,),
            in_specs=[
                pl.BlockSpec((block, 2, levels, fields, degree), lambda i, o, w: (i, 0, 0, 0, 0)),
                pl.BlockSpec((block, lats, degree), lambda i, o, w: (i, 0, 0)),
            ],
            out_specs=pl.BlockSpec((block, lats, channels), lambda i, o, w: (i, 0, 0)),
        ),
        cost_estimate=pl.CostEstimate(
            flops=2 * slots * lats * channels * degree,
            bytes_accessed=2 * slots * degree * (channels + lats),
            transcendentals=0,
        ),
    )(offset, wavenumber, stored, legendre)


def local(spectral, legendre, wavenumber, level_weight, source_row, row_weight):
    slot_count = spectral.shape[0]
    fields = spectral.shape[2]
    levels = spectral.shape[3]
    degree = spectral.shape[4]
    channels = 2 * fields * levels
    wave_count = lax.axis_size("wave")
    cpl_count = lax.axis_size("cpl")
    lev_count = lax.axis_size("lev")
    wave_at = lax.axis_index("wave")
    cpl_at = lax.axis_index("cpl")
    stored = jnp.transpose(spectral, (0, 1, 3, 2, 4))
    spec_grid = legendre_transform(
        stored, legendre, wavenumber, (wave_at * slot_count).astype(jnp.int32).reshape(1)
    )
    by_latitude = lax.all_to_all(spec_grid, "wave", split_axis=1, concat_axis=0, tiled=True)
    total_slots = by_latitude.shape[0]
    lat_dev = by_latitude.shape[1]
    rows = lat_dev * fields * levels
    parts = by_latitude.reshape(total_slots, lat_dev, 2, fields * levels)
    real = parts[:, :, 0].reshape(total_slots, rows).T
    imag = parts[:, :, 1].reshape(total_slots, rows).T
    parity = (1 - 2 * (wavenumber & 1)).astype(jnp.bfloat16)[None, :]
    lhs_cos = jnp.concatenate([real, real * parity], axis=0)
    lhs_sin = jnp.concatenate([imag, imag * parity], axis=0)

    quarter = NLON // 4
    width = -(-(quarter + 1) // LANE) * LANE
    cos_tab, sin_tab = quarter_tables(wavenumber, width)
    r_all = jnp.dot(lhs_cos, cos_tab, preferred_element_type=jnp.float32)
    q_all = jnp.dot(lhs_sin, sin_tab, preferred_element_type=jnp.float32)
    r1, r2 = r_all[:rows], r_all[rows:]
    q1, q2 = q_all[:rows], q_all[rows:]

    def flux_of(grid_rows):
        return surface_flux(grid_rows.reshape(lat_dev, levels, fields, quarter), level_weight)

    strip0 = flux_of((r1 + q1)[:, :quarter])
    strip1 = jnp.flip(flux_of((r2 - q2)[:, 1 : quarter + 1]), axis=-1)
    strip2 = flux_of((r2 + q2)[:, :quarter])
    strip3 = jnp.flip(flux_of((r1 - q1)[:, 1 : quarter + 1]), axis=-1)
    partial_value = jnp.concatenate([strip0, strip1, strip2, strip3], axis=-1)

    own_first = (wave_at * cpl_count + cpl_at) * lat_dev
    source = lax.dynamic_slice_in_dim(source_row, own_first, lat_dev)
    weight_hi = lax.dynamic_slice_in_dim(row_weight, own_first, lat_dev)
    strip_width = NLON // lev_count
    by_strip = partial_value.reshape(lat_dev, fields, lev_count, strip_width).transpose(2, 0, 1, 3)
    summed = jnp.sum(
        lax.all_to_all(by_strip, "lev", split_axis=0, concat_axis=0, tiled=True), axis=0
    )
    copies = jnp.broadcast_to(summed[None], (wave_count * cpl_count,) + summed.shape)
    gathered = lax.all_to_all(copies, ("wave", "cpl"), split_axis=0, concat_axis=0, tiled=True)
    gathered = gathered.reshape((wave_count * cpl_count * lat_dev,) + summed.shape[1:])
    gathered = latitude_order(gathered, wave_count, cpl_count, lat_dev)
    return interpolate(gathered, source, weight_hi)


def solution(mesh):
    placed = (P("wave", None, None, "lev", None), P("wave", "cpl", None), P(), P("lev"), P(), P())
    return jax.shard_map(
        local,
        mesh=mesh,
        in_specs=placed,
        out_specs=P(("wave", "cpl"), None, "lev"),
        check_vma=False,
    )
```

```python
import math

import jax
import jax.numpy as jnp
from jax import lax
from jax.sharding import PartitionSpec as P
from jax.experimental import pallas as pl
from jax.experimental.pallas import tpu as pltpu

NLON = 4320
LANE = 128
SLOT_BLOCK = 64


def phase_angle(phase, lon_total):
    return phase.astype(jnp.float32) * (2.0 * math.pi / lon_total)


def surface_flux(grid_vals, level_weight):
    wind_speed = jnp.sqrt(grid_vals[:, 0] ** 2 + grid_vals[:, 1] ** 2 + 0.25)
    return jnp.sum(level_weight[:, None] * wind_speed[:, None] * grid_vals, axis=2)


def latitude_order(gathered, wave_count, cpl_count, lat_dev):
    trailing = gathered.shape[1:]
    gathered = gathered.reshape((wave_count, cpl_count, lat_dev) + trailing)
    gathered = jnp.swapaxes(gathered, 0, 1)
    return gathered.reshape((wave_count * cpl_count * lat_dev,) + trailing)


def interpolate(gathered, source, weight_hi):
    lower = jnp.take(gathered, source, axis=0)
    upper = jnp.take(gathered, source + 1, axis=0)
    return (1.0 - weight_hi[:, None, None]) * lower + weight_hi[:, None, None] * upper


def quarter_tables(wavenumber, width):
    blocks = width // LANE
    factor = jnp.where(wavenumber == 0, 1.0, 2.0).astype(jnp.float32)[:, None]
    fine_count = 16
    fine = jnp.arange(fine_count, dtype=jnp.int32)
    coarse = jnp.arange(LANE // fine_count, dtype=jnp.int32) * fine_count
    fine_angle = phase_angle(wavenumber[:, None] * fine[None, :] % NLON, NLON)[:, None, :]
    coarse_angle = phase_angle(wavenumber[:, None] * coarse[None, :] % NLON, NLON)[:, :, None]
    fine_cos, fine_sin = jnp.cos(fine_angle), jnp.sin(fine_angle)
    coarse_cos, coarse_sin = jnp.cos(coarse_angle), jnp.sin(coarse_angle)
    base_cos = (coarse_cos * fine_cos - coarse_sin * fine_sin).reshape(-1, 1, LANE)
    base_sin = (coarse_sin * fine_cos + coarse_cos * fine_sin).reshape(-1, 1, LANE)
    starts = jnp.arange(blocks, dtype=jnp.int32) * LANE
    start_angle = phase_angle(wavenumber[:, None] * starts[None, :] % NLON, NLON)
    start_cos = (factor * jnp.cos(start_angle))[:, :, None]
    start_sin = (factor * jnp.sin(start_angle))[:, :, None]
    cos_tab = start_cos * base_cos - start_sin * base_sin
    sin_tab = start_sin * base_cos + start_cos * base_sin
    slots = wavenumber.shape[0]
    return (
        cos_tab.astype(jnp.bfloat16).reshape(slots, width),
        (-sin_tab).astype(jnp.bfloat16).reshape(slots, width),
    )


def legendre_kernel(offset_ref, waves_ref, spec_ref, table_ref, out_ref):
    block = spec_ref.shape[0]
    degree = spec_ref.shape[-1]
    first = offset_ref[0] + pl.program_id(0) * block

    def one_slot(s, carry):
        limit = degree - waves_ref[first + s]
        rows = table_ref[s]
        column = lax.broadcasted_iota(jnp.int32, rows.shape, 1)
        rows = jnp.where(column < limit, rows, jnp.zeros_like(rows))
        coefficient = spec_ref[s].reshape(-1, degree)
        out_ref[s] = lax.dot_general(
            rows, coefficient, (((1,), (1,)), ((), ())), preferred_element_type=jnp.float32
        ).astype(out_ref.dtype)
        return carry

    lax.fori_loop(0, block, one_slot, 0, unroll=True)


def legendre_transform(stored, legendre, wavenumber, offset):
    slots, _, levels, fields, degree = stored.shape
    lats = legendre.shape[1]
    channels = 2 * levels * fields
    block = max(b for b in range(1, SLOT_BLOCK + 1) if slots % b == 0)
    return pl.pallas_call(
        legendre_kernel,
        out_shape=jax.ShapeDtypeStruct((slots, lats, channels), jnp.bfloat16),
        grid_spec=pltpu.PrefetchScalarGridSpec(
            num_scalar_prefetch=2,
            grid=(slots // block,),
            in_specs=[
                pl.BlockSpec((block, 2, levels, fields, degree), lambda i, o, w: (i, 0, 0, 0, 0)),
                pl.BlockSpec((block, lats, degree), lambda i, o, w: (i, 0, 0)),
            ],
            out_specs=pl.BlockSpec((block, lats, channels), lambda i, o, w: (i, 0, 0)),
        ),
        cost_estimate=pl.CostEstimate(
            flops=2 * slots * lats * channels * degree,
            bytes_accessed=2 * slots * degree * (channels + lats),
            transcendentals=0,
        ),
    )(offset, wavenumber, stored, legendre)


def local(spectral, legendre, wavenumber, level_weight, source_row, row_weight):
    slot_count = spectral.shape[0]
    fields = spectral.shape[2]
    levels = spectral.shape[3]
    degree = spectral.shape[4]
    channels = 2 * fields * levels
    wave_count = lax.axis_size("wave")
    cpl_count = lax.axis_size("cpl")
    lev_count = lax.axis_size("lev")
    wave_at = lax.axis_index("wave")
    cpl_at = lax.axis_index("cpl")
    stored = jnp.transpose(spectral, (0, 1, 3, 2, 4))
    spec_grid = (
        legendre_transform(
            stored, legendre, wavenumber, (wave_at * slot_count).astype(jnp.int32).reshape(1)
        )
        .reshape(slot_count, legendre.shape[1], 2, levels, fields)
        .transpose(0, 1, 2, 4, 3)
        .reshape(slot_count, legendre.shape[1], channels)
    )
    by_latitude = lax.all_to_all(spec_grid, "wave", split_axis=1, concat_axis=0, tiled=True)
    total_slots = by_latitude.shape[0]
    lat_dev = by_latitude.shape[1]
    rows = lat_dev * fields * levels
    parts = by_latitude.reshape(total_slots, lat_dev, 2, fields * levels)
    real = parts[:, :, 0].reshape(total_slots, rows).T
    imag = parts[:, :, 1].reshape(total_slots, rows).T
    parity = (1 - 2 * (wavenumber & 1)).astype(jnp.bfloat16)[None, :]
    lhs_cos = jnp.concatenate([real, real * parity], axis=0)
    lhs_sin = jnp.concatenate([imag, imag * parity], axis=0)

    quarter = NLON // 4
    width = -(-(quarter + 1) // LANE) * LANE
    cos_tab, sin_tab = quarter_tables(wavenumber, width)
    r_all = jnp.dot(lhs_cos, cos_tab, preferred_element_type=jnp.float32)
    q_all = jnp.dot(lhs_sin, sin_tab, preferred_element_type=jnp.float32)
    r1, r2 = r_all[:rows], r_all[rows:]
    q1, q2 = q_all[:rows], q_all[rows:]

    def flux_of(grid_rows):
        return surface_flux(grid_rows.reshape(lat_dev, fields, levels, quarter), level_weight)

    strip0 = flux_of((r1 + q1)[:, :quarter])
    strip1 = jnp.flip(flux_of((r2 - q2)[:, 1 : quarter + 1]), axis=-1)
    strip2 = flux_of((r2 + q2)[:, :quarter])
    strip3 = jnp.flip(flux_of((r1 - q1)[:, 1 : quarter + 1]), axis=-1)
    quarters = [strip0, strip1, strip2, strip3]

    own_first = (wave_at * cpl_count + cpl_at) * lat_dev
    source = lax.dynamic_slice_in_dim(source_row, own_first, lat_dev)
    weight_hi = lax.dynamic_slice_in_dim(row_weight, own_first, lat_dev)
    strip_width = NLON // lev_count
    if lev_count == len(quarters):
        by_strip = jnp.stack(quarters)
    else:
        partial_value = jnp.concatenate(quarters, axis=-1)
        by_strip = partial_value.reshape(lat_dev, fields, lev_count, strip_width).transpose(2, 0, 1, 3)
    summed = jnp.sum(
        lax.all_to_all(by_strip, "lev", split_axis=0, concat_axis=0, tiled=True), axis=0
    )
    copies = jnp.broadcast_to(summed[None], (wave_count * cpl_count,) + summed.shape)
    gathered = lax.all_to_all(copies, ("wave", "cpl"), split_axis=0, concat_axis=0, tiled=True)
    gathered = gathered.reshape((wave_count * cpl_count * lat_dev,) + summed.shape[1:])
    gathered = latitude_order(gathered, wave_count, cpl_count, lat_dev)
    return interpolate(gathered, source, weight_hi)


def solution(mesh):
    placed = (P("wave", None, None, "lev", None), P("wave", "cpl", None), P(), P("lev"), P(), P())
    return jax.shard_map(
        local,
        mesh=mesh,
        in_specs=placed,
        out_specs=P(("wave", "cpl"), None, "lev"),
        check_vma=False,
    )
```

```python
import math

import jax
import jax.numpy as jnp
from jax import lax
from jax.sharding import PartitionSpec as P
from jax.experimental import pallas as pl
from jax.experimental.pallas import tpu as pltpu

NLON = 4320
LANE = 128
SLOT_BLOCK = 64


def phase_angle(phase, lon_total):
    return phase.astype(jnp.float32) * (2.0 * math.pi / lon_total)


def surface_flux(grid_vals, level_weight):
    wind_speed = jnp.sqrt(grid_vals[:, 0] ** 2 + grid_vals[:, 1] ** 2 + 0.25)
    return jnp.sum(level_weight[:, None] * wind_speed[:, None] * grid_vals, axis=2)


def latitude_order(gathered, wave_count, cpl_count, lat_dev):
    trailing = gathered.shape[1:]
    gathered = gathered.reshape((wave_count, cpl_count, lat_dev) + trailing)
    gathered = jnp.swapaxes(gathered, 0, 1)
    return gathered.reshape((wave_count * cpl_count * lat_dev,) + trailing)


def interpolate(gathered, source, weight_hi):
    lower = jnp.take(gathered, source, axis=0)
    upper = jnp.take(gathered, source + 1, axis=0)
    return (1.0 - weight_hi[:, None, None]) * lower + weight_hi[:, None, None] * upper


def quarter_tables(wavenumber, width):
    blocks = width // LANE
    factor = jnp.where(wavenumber == 0, 1.0, 2.0).astype(jnp.float32)[:, None]
    fine_count = 16
    fine = jnp.arange(fine_count, dtype=jnp.int32)
    coarse = jnp.arange(LANE // fine_count, dtype=jnp.int32) * fine_count
    fine_angle = phase_angle(wavenumber[:, None] * fine[None, :] % NLON, NLON)[:, None, :]
    coarse_angle = phase_angle(wavenumber[:, None] * coarse[None, :] % NLON, NLON)[:, :, None]
    fine_cos, fine_sin = jnp.cos(fine_angle), jnp.sin(fine_angle)
    coarse_cos, coarse_sin = jnp.cos(coarse_angle), jnp.sin(coarse_angle)
    base_cos = (coarse_cos * fine_cos - coarse_sin * fine_sin).reshape(-1, 1, LANE)
    base_sin = (coarse_sin * fine_cos + coarse_cos * fine_sin).reshape(-1, 1, LANE)
    starts = jnp.arange(blocks, dtype=jnp.int32) * LANE
    start_angle = phase_angle(wavenumber[:, None] * starts[None, :] % NLON, NLON)
    start_cos = (factor * jnp.cos(start_angle))[:, :, None]
    start_sin = (factor * jnp.sin(start_angle))[:, :, None]
    cos_tab = start_cos * base_cos - start_sin * base_sin
    sin_tab = start_sin * base_cos + start_cos * base_sin
    slots = wavenumber.shape[0]
    return (
        cos_tab.astype(jnp.bfloat16).reshape(slots, width),
        (-sin_tab).astype(jnp.bfloat16).reshape(slots, width),
    )


def legendre_kernel(offset_ref, waves_ref, spec_ref, table_ref, out_ref):
    block = spec_ref.shape[0]
    degree = spec_ref.shape[-1]
    first = offset_ref[0] + pl.program_id(0) * block

    def one_slot(s, carry):
        limit = degree - waves_ref[first + s]
        rows = table_ref[s]
        column = lax.broadcasted_iota(jnp.int32, rows.shape, 1)
        rows = jnp.where(column < limit, rows, jnp.zeros_like(rows))
        coefficient = spec_ref[s].reshape(-1, degree)
        out_ref[s] = lax.dot_general(
            rows, coefficient, (((1,), (1,)), ((), ())), preferred_element_type=jnp.float32
        ).astype(out_ref.dtype)
        return carry

    lax.fori_loop(0, block, one_slot, 0, unroll=True)


def legendre_transform(stored, legendre, wavenumber, offset):
    slots, _, levels, fields, degree = stored.shape
    lats = legendre.shape[1]
    channels = 2 * levels * fields
    block = max(b for b in range(1, SLOT_BLOCK + 1) if slots % b == 0)
    return pl.pallas_call(
        legendre_kernel,
        out_shape=jax.ShapeDtypeStruct((slots, lats, channels), jnp.bfloat16),
        grid_spec=pltpu.PrefetchScalarGridSpec(
            num_scalar_prefetch=2,
            grid=(slots // block,),
            in_specs=[
                pl.BlockSpec((block, 2, levels, fields, degree), lambda i, o, w: (i, 0, 0, 0, 0)),
                pl.BlockSpec((block, lats, degree), lambda i, o, w: (i, 0, 0)),
            ],
            out_specs=pl.BlockSpec((block, lats, channels), lambda i, o, w: (i, 0, 0)),
        ),
        cost_estimate=pl.CostEstimate(
            flops=2 * slots * lats * channels * degree,
            bytes_accessed=2 * slots * degree * (channels + lats),
            transcendentals=0,
        ),
    )(offset, wavenumber, stored, legendre)


def local(spectral, legendre, wavenumber, level_weight, source_row, row_weight):
    slot_count = spectral.shape[0]
    fields = spectral.shape[2]
    levels = spectral.shape[3]
    degree = spectral.shape[4]
    channels = 2 * fields * levels
    wave_count = lax.axis_size("wave")
    cpl_count = lax.axis_size("cpl")
    lev_count = lax.axis_size("lev")
    wave_at = lax.axis_index("wave")
    cpl_at = lax.axis_index("cpl")
    stored = jnp.transpose(spectral, (0, 1, 3, 2, 4))
    spec_grid = (
        legendre_transform(
            stored, legendre, wavenumber, (wave_at * slot_count).astype(jnp.int32).reshape(1)
        )
        .reshape(slot_count, legendre.shape[1], 2, levels, fields)
        .transpose(0, 1, 2, 4, 3)
        .reshape(slot_count, legendre.shape[1], channels)
    )
    by_latitude = lax.all_to_all(spec_grid, "wave", split_axis=1, concat_axis=0, tiled=True)
    total_slots = by_latitude.shape[0]
    lat_dev = by_latitude.shape[1]
    rows = lat_dev * fields * levels
    parts = by_latitude.reshape(total_slots, lat_dev, 2, fields * levels)
    real = parts[:, :, 0].reshape(total_slots, rows).T
    imag = parts[:, :, 1].reshape(total_slots, rows).T
    parity = (1 - 2 * (wavenumber & 1)).astype(jnp.bfloat16)[None, :]
    lhs_cos = jnp.concatenate([real, real * parity], axis=0)
    lhs_sin = jnp.concatenate([imag, imag * parity], axis=0)

    quarter = NLON // 4
    width = -(-(quarter + 1) // LANE) * LANE
    cos_tab, sin_tab = quarter_tables(wavenumber, width)
    r_all = jnp.dot(lhs_cos, cos_tab, preferred_element_type=jnp.float32)
    q_all = jnp.dot(lhs_sin, sin_tab, preferred_element_type=jnp.float32)
    r1, r2 = r_all[:rows], r_all[rows:]
    q1, q2 = q_all[:rows], q_all[rows:]

    def flux_of(grid_rows):
        return surface_flux(grid_rows.reshape(lat_dev, fields, levels, quarter), level_weight)

    strip0 = flux_of((r1 + q1)[:, :quarter])
    mirror1 = flux_of((r2 - q2)[:, 1 : quarter + 1])
    strip2 = flux_of((r2 + q2)[:, :quarter])
    mirror3 = flux_of((r1 - q1)[:, 1 : quarter + 1])
    quarters = [strip0, jnp.flip(mirror1, axis=-1), strip2, jnp.flip(mirror3, axis=-1)]

    own_first = (wave_at * cpl_count + cpl_at) * lat_dev
    source = lax.dynamic_slice_in_dim(source_row, own_first, lat_dev)
    weight_hi = lax.dynamic_slice_in_dim(row_weight, own_first, lat_dev)
    strip_width = NLON // lev_count
    if lev_count == len(quarters):
        by_strip = jnp.stack([strip0, mirror1, strip2, mirror3])
    else:
        partial_value = jnp.concatenate(quarters, axis=-1)
        by_strip = partial_value.reshape(lat_dev, fields, lev_count, strip_width).transpose(2, 0, 1, 3)
    summed = jnp.sum(
        lax.all_to_all(by_strip, "lev", split_axis=0, concat_axis=0, tiled=True), axis=0
    )
    copies = jnp.broadcast_to(summed[None], (wave_count * cpl_count,) + summed.shape)
    gathered = lax.all_to_all(copies, ("wave", "cpl"), split_axis=0, concat_axis=0, tiled=True)
    gathered = gathered.reshape((wave_count * cpl_count * lat_dev,) + summed.shape[1:])
    gathered = latitude_order(gathered, wave_count, cpl_count, lat_dev)
    result = interpolate(gathered, source, weight_hi)
    if lev_count == len(quarters):
        mirrored = lax.axis_index("lev") % 2 == 1
        result = jnp.where(mirrored, jnp.flip(result, axis=-1), result)
    return result


def solution(mesh):
    placed = (P("wave", None, None, "lev", None), P("wave", "cpl", None), P(), P("lev"), P(), P())
    return jax.shard_map(
        local,
        mesh=mesh,
        in_specs=placed,
        out_specs=P(("wave", "cpl"), None, "lev"),
        check_vma=False,
    )
```

```python
import math

import jax
import jax.numpy as jnp
from jax import lax
from jax.sharding import PartitionSpec as P
from jax.experimental import pallas as pl
from jax.experimental.pallas import tpu as pltpu

NLON = 4320
LANE = 128
SLOT_BLOCK = 80


def phase_angle(phase, lon_total):
    return phase.astype(jnp.float32) * (2.0 * math.pi / lon_total)


def surface_flux(grid_vals, level_weight):
    wind_speed = jnp.sqrt(grid_vals[:, 0] ** 2 + grid_vals[:, 1] ** 2 + 0.25)
    return jnp.sum(level_weight[:, None] * wind_speed[:, None] * grid_vals, axis=2)


def latitude_order(gathered, wave_count, cpl_count, lat_dev):
    trailing = gathered.shape[1:]
    gathered = gathered.reshape((wave_count, cpl_count, lat_dev) + trailing)
    gathered = jnp.swapaxes(gathered, 0, 1)
    return gathered.reshape((wave_count * cpl_count * lat_dev,) + trailing)


def interpolate(gathered, source, weight_hi):
    lower = jnp.take(gathered, source, axis=0)
    upper = jnp.take(gathered, source + 1, axis=0)
    return (1.0 - weight_hi[:, None, None]) * lower + weight_hi[:, None, None] * upper


def quarter_tables(wavenumber, width):
    blocks = width // LANE
    factor = jnp.where(wavenumber == 0, 1.0, 2.0).astype(jnp.float32)[:, None]
    fine_count = 16
    fine = jnp.arange(fine_count, dtype=jnp.int32)
    coarse = jnp.arange(LANE // fine_count, dtype=jnp.int32) * fine_count
    fine_angle = phase_angle(wavenumber[:, None] * fine[None, :] % NLON, NLON)[:, None, :]
    coarse_angle = phase_angle(wavenumber[:, None] * coarse[None, :] % NLON, NLON)[:, :, None]
    fine_cos, fine_sin = jnp.cos(fine_angle), jnp.sin(fine_angle)
    coarse_cos, coarse_sin = jnp.cos(coarse_angle), jnp.sin(coarse_angle)
    base_cos = (coarse_cos * fine_cos - coarse_sin * fine_sin).reshape(-1, 1, LANE)
    base_sin = (coarse_sin * fine_cos + coarse_cos * fine_sin).reshape(-1, 1, LANE)
    starts = jnp.arange(blocks, dtype=jnp.int32) * LANE
    start_angle = phase_angle(wavenumber[:, None] * starts[None, :] % NLON, NLON)
    start_cos = (factor * jnp.cos(start_angle))[:, :, None]
    start_sin = (factor * jnp.sin(start_angle))[:, :, None]
    cos_tab = start_cos * base_cos - start_sin * base_sin
    sin_tab = start_sin * base_cos + start_cos * base_sin
    slots = wavenumber.shape[0]
    return (
        cos_tab.astype(jnp.bfloat16).reshape(slots, width),
        (-sin_tab).astype(jnp.bfloat16).reshape(slots, width),
    )


def legendre_kernel(offset_ref, waves_ref, spec_ref, table_ref, out_ref):
    block = spec_ref.shape[0]
    degree = spec_ref.shape[-1]
    first = offset_ref[0] + pl.program_id(0) * block

    def one_slot(s, carry):
        limit = degree - waves_ref[first + s]
        rows = table_ref[s]
        column = lax.broadcasted_iota(jnp.int32, rows.shape, 1)
        rows = jnp.where(column < limit, rows, jnp.zeros_like(rows))
        coefficient = spec_ref[s].reshape(-1, degree)
        out_ref[s] = lax.dot_general(
            rows, coefficient, (((1,), (1,)), ((), ())), preferred_element_type=jnp.float32
        ).astype(out_ref.dtype)
        return carry

    lax.fori_loop(0, block, one_slot, 0, unroll=True)


def legendre_transform(stored, legendre, wavenumber, offset):
    slots, _, levels, fields, degree = stored.shape
    lats = legendre.shape[1]
    channels = 2 * levels * fields
    block = max(b for b in range(1, SLOT_BLOCK + 1) if slots % b == 0)
    return pl.pallas_call(
        legendre_kernel,
        out_shape=jax.ShapeDtypeStruct((slots, lats, channels), jnp.bfloat16),
        grid_spec=pltpu.PrefetchScalarGridSpec(
            num_scalar_prefetch=2,
            grid=(slots // block,),
            in_specs=[
                pl.BlockSpec((block, 2, levels, fields, degree), lambda i, o, w: (i, 0, 0, 0, 0)),
                pl.BlockSpec((block, lats, degree), lambda i, o, w: (i, 0, 0)),
            ],
            out_specs=pl.BlockSpec((block, lats, channels), lambda i, o, w: (i, 0, 0)),
        ),
        cost_estimate=pl.CostEstimate(
            flops=2 * slots * lats * channels * degree,
            bytes_accessed=2 * slots * degree * (channels + lats),
            transcendentals=0,
        ),
    )(offset, wavenumber, stored, legendre)


def local(spectral, legendre, wavenumber, level_weight, source_row, row_weight):
    slot_count = spectral.shape[0]
    fields = spectral.shape[2]
    levels = spectral.shape[3]
    degree = spectral.shape[4]
    channels = 2 * fields * levels
    wave_count = lax.axis_size("wave")
    cpl_count = lax.axis_size("cpl")
    lev_count = lax.axis_size("lev")
    wave_at = lax.axis_index("wave")
    cpl_at = lax.axis_index("cpl")
    stored = jnp.transpose(spectral, (0, 1, 3, 2, 4))
    spec_grid = (
        legendre_transform(
            stored, legendre, wavenumber, (wave_at * slot_count).astype(jnp.int32).reshape(1)
        )
        .reshape(slot_count, legendre.shape[1], 2, levels, fields)
        .transpose(0, 1, 2, 4, 3)
        .reshape(slot_count, legendre.shape[1], channels)
    )
    by_latitude = lax.all_to_all(spec_grid, "wave", split_axis=1, concat_axis=0, tiled=True)
    total_slots = by_latitude.shape[0]
    lat_dev = by_latitude.shape[1]
    rows = lat_dev * fields * levels
    parts = by_latitude.reshape(total_slots, lat_dev, 2, fields * levels)
    real = parts[:, :, 0].reshape(total_slots, rows).T
    imag = parts[:, :, 1].reshape(total_slots, rows).T
    parity = (1 - 2 * (wavenumber & 1)).astype(jnp.bfloat16)[None, :]
    lhs_cos = jnp.concatenate([real, real * parity], axis=0)
    lhs_sin = jnp.concatenate([imag, imag * parity], axis=0)

    quarter = NLON // 4
    width = -(-(quarter + 1) // LANE) * LANE
    cos_tab, sin_tab = quarter_tables(wavenumber, width)
    r_all = jnp.dot(lhs_cos, cos_tab, preferred_element_type=jnp.float32)
    q_all = jnp.dot(lhs_sin, sin_tab, preferred_element_type=jnp.float32)
    r1, r2 = r_all[:rows], r_all[rows:]
    q1, q2 = q_all[:rows], q_all[rows:]

    def flux_of(grid_rows):
        return surface_flux(grid_rows.reshape(lat_dev, fields, levels, quarter), level_weight)

    strip0 = flux_of((r1 + q1)[:, :quarter])
    mirror1 = flux_of((r2 - q2)[:, 1 : quarter + 1])
    strip2 = flux_of((r2 + q2)[:, :quarter])
    mirror3 = flux_of((r1 - q1)[:, 1 : quarter + 1])
    quarters = [strip0, jnp.flip(mirror1, axis=-1), strip2, jnp.flip(mirror3, axis=-1)]

    own_first = (wave_at * cpl_count + cpl_at) * lat_dev
    source = lax.dynamic_slice_in_dim(source_row, own_first, lat_dev)
    weight_hi = lax.dynamic_slice_in_dim(row_weight, own_first, lat_dev)
    strip_width = NLON // lev_count
    if lev_count == len(quarters):
        by_strip = jnp.stack([strip0, mirror1, strip2, mirror3])
    else:
        partial_value = jnp.concatenate(quarters, axis=-1)
        by_strip = partial_value.reshape(lat_dev, fields, lev_count, strip_width).transpose(2, 0, 1, 3)
    summed = jnp.sum(
        lax.all_to_all(by_strip, "lev", split_axis=0, concat_axis=0, tiled=True), axis=0
    )
    copies = jnp.broadcast_to(summed[None], (wave_count * cpl_count,) + summed.shape)
    gathered = lax.all_to_all(copies, ("wave", "cpl"), split_axis=0, concat_axis=0, tiled=True)
    gathered = gathered.reshape((wave_count * cpl_count * lat_dev,) + summed.shape[1:])
    gathered = latitude_order(gathered, wave_count, cpl_count, lat_dev)
    result = interpolate(gathered, source, weight_hi)
    if lev_count == len(quarters):
        mirrored = lax.axis_index("lev") % 2 == 1
        result = jnp.where(mirrored, jnp.flip(result, axis=-1), result)
    return result


def solution(mesh):
    placed = (P("wave", None, None, "lev", None), P("wave", "cpl", None), P(), P("lev"), P(), P())
    return jax.shard_map(
        local,
        mesh=mesh,
        in_specs=placed,
        out_specs=P(("wave", "cpl"), None, "lev"),
        check_vma=False,
    )
```
